512 devices in a mesh: cent: 16 (over z), blk: 32 (over x, y, core).
Axes of the slice: x: 4, y: 4, z: 16, core: 2. Of those that a mesh axis runs over, the one named last changes fastest.
Arguments:
- query_tokens: bfloat16 [512, 128], replicated, may hold values from -6 to 6
- centroids: bfloat16 [262144, 128], P(('cent', 'blk')), may hold values from -0.5 to 0.5
- tile_ids: int32 [512, 16, 8], P('blk', 'cent'), may hold values from 0 to 127
- tile_count: int32 [512, 16], P('blk', 'cent'), may hold values from 1 to 8
- tile_mask: int32 [512, 16, 8, 128], P('blk', 'cent'), may hold values from 0 to 1, as said below
Outputs:
- block_bound: float32 [16, 512], P(None, 'blk')
The draws below stay inside these ranges and needn't reach their ends.
Inputs may be any that keep to these rules, and one draw needn't show every extreme that they name: `tile_count`: slots at or beyond a block's count are padding; listed tiles may repeat. `tile_mask`: every block has at least one marked lane in a live slot.
All inputs are finite; a program needn't handle non-finite values.
Results may differ from the reference program's by a relative error of at most 0.0006.
Values may be sent and summed in bfloat16 or wider, within the bound.
No kernel may reach another device: no remote copies, remote signals or barrier semaphores. Data moves between devices by JAX's collectives and lax.ppermute only.
A program may use at most 128 MiB of HBM per device.

```python
import jax
import jax.numpy as jnp
from jax import lax

DIM = 128
CENT_DEV = 512
QLEN = 32
QRY = 16
KC = 8
NC = 262144
TPC = 128
QT = 512
NB = 512
N_CENT = 16
N_BLK = 32


def draw_tile_mask(key, part):
    shape = (NB, N_CENT, KC, 128)
    small_shape = (NB, N_CENT, KC, 1)
    first_lane = jax.random.randint(jax.random.fold_in(key, 11), small_shape, 0, 128)
    second_lane = jax.random.randint(jax.random.fold_in(key, 12), small_shape, 0, 128)
    first_live = jax.random.randint(jax.random.fold_in(key, 13), small_shape, 0, N_CENT * KC) < 8
    second_live = jax.random.randint(jax.random.fold_in(key, 14), small_shape, 0, 4 * N_CENT * KC) < 8
    forced_slice = jax.random.randint(jax.random.fold_in(key, 15), (NB, 1, 1, 1), 0, N_CENT)
    lane = lax.broadcasted_iota(jnp.int32, shape, 3)
    slice_pos = lax.broadcasted_iota(jnp.int32, shape, 1)
    slot_pos = lax.broadcasted_iota(jnp.int32, shape, 2)
    forced = (slice_pos == forced_slice) & (slot_pos == 0)
    marked = (lane == first_lane) & (first_live | forced) | (lane == second_lane) & second_live
    return marked.astype(jnp.int32)


def touch_ends(entries, rng, smallest, high):
    place = [jax.random.randint(jax.random.fold_in(rng, axis), (), 0, length) for axis, length in enumerate(entries.shape)]
    longest = entries.shape.index(max(entries.shape))
    next_to = place[:longest] + [(place[longest] + 1) % entries.shape[longest]] + place[longest + 1:]
    return entries.at[tuple(place)].set(smallest).at[tuple(next_to)].set(high)


def steps_of(key, dims, pieces, least, top_value):
    loudness = 1.0
    for dim, parts in pieces:
        steps = jax.random.uniform(jax.random.fold_in(jax.random.fold_in(key, 6), dim), (parts,), jnp.float32, least / len(pieces), top_value / len(pieces))
        loudness = loudness * jnp.repeat(jnp.exp(steps), dims[dim] // parts).reshape((-1,) + (1,) * (len(dims) - 1 - dim))
    return loudness


def centred(rng, shape, scale, bound, cuts=(), held_as=jnp.bfloat16):
    drawn = jax.random.normal(rng, shape, jnp.float32) * scale
    if len(cuts) > 0:
        drawn = steps_of(rng, shape, cuts, -0.22, 0.18) * drawn
    return jnp.clip(drawn, min=-bound, max=bound).astype(held_as)


def setup_inputs(seed: int = 0) -> dict:
    arg_keys = jax.random.split(jax.random.key(seed), 6)
    query_tokens = centred(arg_keys[0], (QT, DIM), 1.0, 6.0)
    centroids = centred(arg_keys[1], (NC, DIM), DIM ** -0.5, 0.5, ((0, 512),))
    tile_ids = touch_ends(jax.random.randint(arg_keys[2], (NB, N_CENT, KC), 0, TPC), jax.random.fold_in(arg_keys[2], 1), 0, TPC - 1).astype(jnp.int32)
    tile_count = touch_ends(jax.random.randint(arg_keys[3], (NB, N_CENT), 1, KC + 1), jax.random.fold_in(arg_keys[3], 1), 1, KC).astype(jnp.int32)
    tile_mask = draw_tile_mask(jax.random.fold_in(arg_keys[5], 71), 0)
    return dict(query_tokens=query_tokens, centroids=centroids, tile_ids=tile_ids, tile_count=tile_count, tile_mask=tile_mask)


def reference(query_tokens, centroids, tile_ids, tile_count, tile_mask):
    span_size = CENT_DEV * N_BLK
    block_total = tile_ids.shape[0]
    slot_count = tile_ids.shape[2]
    floor_value = jnp.array(-jnp.inf, jnp.bfloat16)
    running = jnp.full((QRY, QLEN, block_total), floor_value, jnp.bfloat16)
    position = lax.broadcasted_iota(jnp.int32, (block_total, slot_count, 128), 1)
    for slice_index in range(N_CENT):
        chosen = centroids[slice_index * span_size:(slice_index + 1) * span_size]
        slice_scores = jnp.dot(query_tokens, chosen.T, preferred_element_type=jnp.float32).astype(jnp.bfloat16)
        tile_scores = slice_scores.reshape(QRY, QLEN, span_size // 128, 128)
        flat_ids = tile_ids[:, slice_index, :].reshape(block_total * slot_count).astype(jnp.int32)
        live_lanes = (tile_mask[:, slice_index] > 0) & (position < tile_count[:, slice_index][:, None, None])

        def query_max(query_rows):
            picked = jnp.take(query_rows, flat_ids, axis=1).reshape(QLEN, block_total, slot_count, 128)
            return jnp.max(jnp.where(live_lanes[None], picked, floor_value), axis=(2, 3))

        running = jnp.maximum(running, lax.map(query_max, tile_scores))
    return jnp.mean(running.astype(jnp.float32), axis=1)
```

```python
import jax
import jax.numpy as jnp
from jax import lax
from jax.experimental import pallas as pl
from jax.experimental.pallas import tpu as pltpu
from jax.sharding import PartitionSpec as P

QLEN = 32
QRY = 16
LANES = 128


def block_max_kernel(ids_ref, cnt_ref, q_ref, c_ref, m_ref, o_ref, run_ref):
    nb, ns = m_ref.shape[0], m_ref.shape[1]
    tokens = q_ref.shape[0]
    tiles = c_ref.shape[0] // LANES
    q = q_ref[...]
    lane = lax.broadcasted_iota(jnp.int32, (tokens, nb), 1)

    def body(b, acc):
        cnt = cnt_ref[b]
        run_ref[...] = jnp.full(run_ref.shape, -jnp.inf, jnp.float32)
        for k in range(ns):
            @pl.when(k < cnt)
            def _():
                tid = jnp.clip(ids_ref[b * ns + k], 0, tiles - 1)
                start = pl.multiple_of(tid * LANES, LANES)
                tile = c_ref[pl.ds(start, LANES), :]
                s = lax.dot_general(q, tile, (((1,), (1,)), ((), ())),
                                    preferred_element_type=jnp.float32)
                s = s.astype(jnp.bfloat16).astype(jnp.float32)
                live = m_ref[b, pl.ds(k, 1), :] > 0
                run_ref[...] = jnp.maximum(run_ref[...], jnp.where(live, s, -jnp.inf))
        col = jnp.max(run_ref[...], axis=1, keepdims=True)
        return jnp.where(lane == b, col, acc)

    acc = lax.fori_loop(0, nb, body, jnp.full((tokens, nb), -jnp.inf, jnp.float32))
    o_ref[...] = acc


def block_max(query_tokens, cent_slice, tile_ids, tile_count, tile_mask):
    nb, ns = tile_ids.shape
    tokens = query_tokens.shape[0]
    flops = 2 * tokens * query_tokens.shape[1] * nb * ns * LANES
    return pl.pallas_call(
        block_max_kernel,
        out_shape=jax.ShapeDtypeStruct((tokens, nb), jnp.float32),
        in_specs=[
            pl.BlockSpec(memory_space=pltpu.SMEM),
            pl.BlockSpec(memory_space=pltpu.SMEM),
            pl.BlockSpec(memory_space=pltpu.VMEM),
            pl.BlockSpec(memory_space=pltpu.VMEM),
            pl.BlockSpec(memory_space=pltpu.VMEM),
        ],
        out_specs=pl.BlockSpec(memory_space=pltpu.VMEM),
        scratch_shapes=[pltpu.VMEM((tokens, LANES), jnp.float32)],
        compiler_params=pltpu.CompilerParams(vmem_limit_bytes=48 * 1024 * 1024),
        cost_estimate=pl.CostEstimate(
            flops=flops, transcendentals=0,
            bytes_accessed=cent_slice.size * 2 + query_tokens.size * 2 + tile_mask.size * 4),
    )(tile_ids.reshape(nb * ns), tile_count, query_tokens, cent_slice, tile_mask)


def local(query_tokens, centroids, tile_ids, tile_count, tile_mask):
    nb, ns = tile_ids.shape[0], tile_ids.shape[2]
    cent_slice = lax.all_gather(centroids, "blk", axis=0, tiled=True)
    token_max = block_max(
        query_tokens,
        cent_slice,
        tile_ids.reshape(nb, ns),
        tile_count.reshape(nb),
        tile_mask.reshape(nb, ns, LANES),
    ).astype(jnp.bfloat16)
    every = lax.all_gather(token_max, "cent", axis=0, tiled=False)
    full_max = jnp.max(every, axis=0)
    per_query = full_max.astype(jnp.float32).reshape(QRY, QLEN, nb)
    return jnp.mean(per_query, axis=1)


def solution(mesh):
    in_specs = (
        P(),
        P(("cent", "blk"), None),
        P("blk", "cent", None),
        P("blk", "cent"),
        P("blk", "cent", None, None),
    )
    out_specs = P(None, "blk")
    return jax.shard_map(local, mesh=mesh, in_specs=in_specs, out_specs=out_specs, check_vma=False)
```

```python
import jax
import jax.numpy as jnp
from jax import lax
from jax.experimental import pallas as pl
from jax.experimental.pallas import tpu as pltpu
from jax.sharding import Mesh
from jax.sharding import PartitionSpec as P

QLEN = 32
QRY = 16
LANES = 128
CHIP_X = 4
CHIP_Y = 4
CORES = 2


def block_max_kernel(ids_ref, live_ref, core_ref, q_ref, own_ref, other_ref, m_ref, o_ref, run_ref):
    nb, ns = m_ref.shape[0], m_ref.shape[1]
    tokens = q_ref.shape[0]
    chips, rows = own_ref.shape[0], own_ref.shape[1]
    per_dev = rows // LANES
    tiles = chips * CORES * per_dev
    core = core_ref[0]
    q = q_ref[...]
    lane = lax.broadcasted_iota(jnp.int32, (tokens, nb), 1)

    def update(src, chip, start, b, k):
        tile = src[chip, pl.ds(start, LANES), :]
        s = lax.dot_general(q, tile, (((1,), (1,)), ((), ())),
                            preferred_element_type=jnp.float32)
        s = s.astype(jnp.bfloat16).astype(jnp.float32)
        live = m_ref[b, pl.ds(k, 1), :] > 0
        run_ref[...] = jnp.maximum(run_ref[...], jnp.where(live, s, -jnp.inf))

    def body(b, acc):
        run_ref[...] = jnp.full(run_ref.shape, -jnp.inf, jnp.float32)
        for k in range(ns):
            @pl.when(live_ref[b * ns + k] > 0)
            def _():
                tid = jnp.clip(ids_ref[b * ns + k], 0, tiles - 1)
                dev = tid // per_dev
                chip = dev // CORES
                start = pl.multiple_of((tid % per_dev) * LANES, LANES)

                @pl.when(dev % CORES == core)
                def _():
                    update(own_ref, chip, start, b, k)

                @pl.when(dev % CORES != core)
                def _():
                    update(other_ref, chip, start, b, k)

        col = jnp.max(run_ref[...], axis=1, keepdims=True)
        return jnp.where(lane == b, col, acc)

    acc = lax.fori_loop(0, nb, body, jnp.full((tokens, nb), -jnp.inf, jnp.float32))
    o_ref[...] = acc


def block_max(query_tokens, own, other, core, tile_ids, slot_live, tile_mask):
    nb, ns = tile_ids.shape
    tokens = query_tokens.shape[0]
    flops = 2 * tokens * query_tokens.shape[1] * nb * ns * LANES
    return pl.pallas_call(
        block_max_kernel,
        out_shape=jax.ShapeDtypeStruct((tokens, nb), jnp.float32),
        in_specs=[
            pl.BlockSpec(memory_space=pltpu.SMEM),
            pl.BlockSpec(memory_space=pltpu.SMEM),
            pl.BlockSpec(memory_space=pltpu.SMEM),
            pl.BlockSpec(memory_space=pltpu.VMEM),
            pl.BlockSpec(memory_space=pltpu.VMEM),
            pl.BlockSpec(memory_space=pltpu.VMEM),
            pl.BlockSpec(memory_space=pltpu.VMEM),
        ],
        out_specs=pl.BlockSpec(memory_space=pltpu.VMEM),
        scratch_shapes=[pltpu.VMEM((tokens, LANES), jnp.float32)],
        compiler_params=pltpu.CompilerParams(vmem_limit_bytes=48 * 1024 * 1024),
        cost_estimate=pl.CostEstimate(
            flops=flops, transcendentals=0,
            bytes_accessed=2 * own.size * 2 + query_tokens.size * 2 + tile_mask.size * 4),
    )(tile_ids.reshape(nb * ns), slot_live.reshape(nb * ns), core, query_tokens, own, other, tile_mask)


def local(query_tokens, centroids, tile_ids, tile_count, tile_mask):
    nb, ns = tile_ids.shape[0], tile_ids.shape[2]
    rows = centroids.shape[0]
    chips = CHIP_X * CHIP_Y
    core = lax.axis_index("core")
    spread = jnp.broadcast_to(centroids[None], (chips, rows, centroids.shape[1]))
    own = lax.all_to_all(spread, ("x", "y"), 0, 0, tiled=False)
    other = lax.ppermute(own, "core", [(0, 1), (1, 0)])
    mask = tile_mask.reshape(nb, ns, LANES)
    slot = lax.broadcasted_iota(jnp.int32, (nb, ns), 1)
    slot_live = ((slot < tile_count.reshape(nb, 1)) & jnp.any(mask > 0, axis=2)).astype(jnp.int32)
    token_max = block_max(
        query_tokens, own, other, core.reshape(1).astype(jnp.int32),
        tile_ids.reshape(nb, ns), slot_live, mask,
    ).astype(jnp.bfloat16)
    tokens = token_max.shape[0]
    dense = token_max.reshape(tokens * nb // LANES, LANES)
    n_cent = lax.axis_size("cent")
    every = lax.all_to_all(jnp.broadcast_to(dense[None], (n_cent,) + dense.shape), "cent", 0, 0, tiled=False)
    full_max = jnp.max(every, axis=0).reshape(tokens, nb)
    per_query = full_max.astype(jnp.float32).reshape(QRY, QLEN, nb)
    return jnp.mean(per_query, axis=1)


def solution(mesh):
    n_cent = mesh.shape["cent"]
    split = Mesh(mesh.devices.reshape(n_cent, CHIP_X, CHIP_Y, CORES), ("cent", "x", "y", "core"))
    blk = ("x", "y", "core")
    in_specs = (
        P(),
        P(("cent",) + blk, None),
        P(blk, "cent", None),
        P(blk, "cent"),
        P(blk, "cent", None, None),
    )
    out_specs = P(None, blk)
    return jax.shard_map(local, mesh=split, in_specs=in_specs, out_specs=out_specs, check_vma=False)
```

```python
import jax
import jax.numpy as jnp
from jax import lax
from jax.experimental import pallas as pl
from jax.experimental.pallas import tpu as pltpu
from jax.sharding import Mesh
from jax.sharding import PartitionSpec as P

QLEN = 32
QRY = 16
LANES = 128
CHIP_X = 4
CHIP_Y = 4
CORES = 2


def block_max_kernel(ids_ref, use_ref, has_ref, q_ref, own_ref, m_ref, o_ref, run_ref):
    nb, ns = m_ref.shape[0], m_ref.shape[1]
    tokens = q_ref.shape[0]
    chips, rows = own_ref.shape[0], own_ref.shape[1]
    per_dev = rows // LANES
    tiles = chips * CORES * per_dev
    q = q_ref[...]
    lane = lax.broadcasted_iota(jnp.int32, (tokens, nb), 1)
    o_ref[...] = jnp.full(o_ref.shape, -jnp.inf, jnp.float32)

    def body(b, carry):
        @pl.when(has_ref[b] > 0)
        def _():
            run_ref[...] = jnp.full(run_ref.shape, -jnp.inf, jnp.float32)
            for k in range(ns):
                @pl.when(use_ref[b * ns + k] > 0)
                def _():
                    tid = jnp.clip(ids_ref[b * ns + k], 0, tiles - 1)
                    chip = (tid // per_dev) // CORES
                    start = pl.multiple_of((tid % per_dev) * LANES, LANES)
                    tile = own_ref[chip, pl.ds(start, LANES), :]
                    s = lax.dot_general(q, tile, (((1,), (1,)), ((), ())),
                                        preferred_element_type=jnp.float32)
                    s = s.astype(jnp.bfloat16).astype(jnp.float32)
                    live = m_ref[b, pl.ds(k, 1), :] > 0
                    run_ref[...] = jnp.maximum(run_ref[...], jnp.where(live, s, -jnp.inf))

            col = jnp.max(run_ref[...], axis=1, keepdims=True)
            o_ref[...] = jnp.where(lane == b, col, o_ref[...])

        return carry

    lax.fori_loop(0, nb, body, 0)


def block_max(query_tokens, own, tile_ids, slot_use, block_has, tile_mask):
    nb, ns = tile_ids.shape
    tokens = query_tokens.shape[0]
    flops = tokens * query_tokens.shape[1] * nb * ns * LANES
    return pl.pallas_call(
        block_max_kernel,
        out_shape=jax.ShapeDtypeStruct((tokens, nb), jnp.float32),
        in_specs=[
            pl.BlockSpec(memory_space=pltpu.SMEM),
            pl.BlockSpec(memory_space=pltpu.SMEM),
            pl.BlockSpec(memory_space=pltpu.SMEM),
            pl.BlockSpec(memory_space=pltpu.VMEM),
            pl.BlockSpec(memory_space=pltpu.VMEM),
            pl.BlockSpec(memory_space=pltpu.VMEM),
        ],
        out_specs=pl.BlockSpec(memory_space=pltpu.VMEM),
        scratch_shapes=[pltpu.VMEM((tokens, LANES), jnp.float32)],
        compiler_params=pltpu.CompilerParams(vmem_limit_bytes=48 * 1024 * 1024),
        cost_estimate=pl.CostEstimate(
            flops=flops, transcendentals=0,
            bytes_accessed=own.size * 2 + query_tokens.size * 2 + tile_mask.size * 4),
    )(tile_ids.reshape(nb * ns), slot_use.reshape(nb * ns), block_has, query_tokens, own, tile_mask)


def local(query_tokens, centroids, tile_ids, tile_count, tile_mask):
    nb, ns = tile_ids.shape[0], tile_ids.shape[2]
    rows = centroids.shape[0]
    per_dev = rows // LANES
    chips = CHIP_X * CHIP_Y
    core = lax.axis_index("core")
    ids = tile_ids.reshape(nb, ns)
    mask = tile_mask.reshape(nb, ns, LANES)
    slot = lax.broadcasted_iota(jnp.int32, (nb, ns), 1)
    live = ((slot < tile_count.reshape(nb, 1)) & jnp.any(mask > 0, axis=2)).astype(jnp.int32)
    p_ids, p_live, p_mask = lax.ppermute((ids, live, mask), "core", [(0, 1), (1, 0)])
    first = core == 0
    all_ids = jnp.where(first, jnp.concatenate([ids, p_ids]), jnp.concatenate([p_ids, ids]))
    all_live = jnp.where(first, jnp.concatenate([live, p_live]), jnp.concatenate([p_live, live]))
    all_mask = jnp.where(first, jnp.concatenate([mask, p_mask]), jnp.concatenate([p_mask, mask]))
    owner = (jnp.clip(all_ids, 0, chips * CORES * per_dev - 1) // per_dev) % CORES
    use = ((all_live > 0) & (owner == core)).astype(jnp.int32)
    has = jnp.max(use, axis=1)
    spread = jnp.broadcast_to(centroids[None], (chips, rows, centroids.shape[1]))
    own = lax.all_to_all(spread, ("x", "y"), 0, 0, tiled=False)
    partial = block_max(query_tokens, own, all_ids, use, has, all_mask).astype(jnp.bfloat16)
    tokens = partial.shape[0]
    per_core = partial.reshape(tokens, CORES, nb).transpose(1, 0, 2).reshape(CORES, tokens * nb // LANES, LANES)
    n_cent = lax.axis_size("cent")
    send = jnp.broadcast_to(per_core[None], (n_cent,) + per_core.shape).reshape((n_cent * CORES,) + per_core.shape[1:])
    every = lax.all_to_all(send, ("cent", "core"), 0, 0, tiled=False)
    full_max = jnp.max(every, axis=0).reshape(tokens, nb)
    per_query = full_max.astype(jnp.float32).reshape(QRY, QLEN, nb)
    return jnp.mean(per_query, axis=1)


def solution(mesh):
    n_cent = mesh.shape["cent"]
    split = Mesh(mesh.devices.reshape(n_cent, CHIP_X, CHIP_Y, CORES), ("cent", "x", "y", "core"))
    blk = ("x", "y", "core")
    in_specs = (
        P(),
        P(("cent",) + blk, None),
        P(blk, "cent", None),
        P(blk, "cent"),
        P(blk, "cent", None, None),
    )
    out_specs = P(None, blk)
    return jax.shard_map(local, mesh=split, in_specs=in_specs, out_specs=out_specs, check_vma=False)
```

```python
import jax
import jax.numpy as jnp
from jax import lax
from jax.experimental import pallas as pl
from jax.experimental.pallas import tpu as pltpu
from jax.sharding import Mesh
from jax.sharding import PartitionSpec as P

QLEN = 32
QRY = 16
LANES = 128
CHIP_X = 4
CHIP_Y = 4
CORES = 2


def block_max_kernel(ids_ref, use_ref, has_ref, q_ref, own_ref, m_ref, o_ref, run_ref):
    nb, ns = m_ref.shape[0], m_ref.shape[1]
    tokens = q_ref.shape[0]
    chips, rows = own_ref.shape[0], own_ref.shape[1]
    per_dev = rows // LANES
    tiles = chips * CORES * per_dev
    q = q_ref[...]
    lane = lax.broadcasted_iota(jnp.int32, (tokens, nb), 1)
    o_ref[...] = jnp.full(o_ref.shape, -jnp.inf, jnp.float32)

    def body(b, carry):
        @pl.when(has_ref[b] > 0)
        def _():
            run_ref[...] = jnp.full(run_ref.shape, -jnp.inf, jnp.float32)
            for k in range(ns):
                @pl.when(use_ref[b * ns + k] > 0)
                def _():
                    tid = jnp.clip(ids_ref[b * ns + k], 0, tiles - 1)
                    chip = (tid // per_dev) // CORES
                    start = pl.multiple_of((tid % per_dev) * LANES, LANES)
                    tile = own_ref[chip, pl.ds(start, LANES), :]
                    s = lax.dot_general(q, tile, (((1,), (1,)), ((), ())),
                                        preferred_element_type=jnp.float32)
                    s = s.astype(jnp.bfloat16).astype(jnp.float32)
                    live = m_ref[b, pl.ds(k, 1), :] > 0
                    run_ref[...] = jnp.maximum(run_ref[...], jnp.where(live, s, -jnp.inf))

            col = jnp.max(run_ref[...], axis=1, keepdims=True)
            o_ref[...] = jnp.where(lane == b, col, o_ref[...])

        return carry

    lax.fori_loop(0, nb, body, 0)


def block_max(query_tokens, own, tile_ids, slot_use, block_has, tile_mask):
    nb, ns = tile_ids.shape
    tokens = query_tokens.shape[0]
    flops = tokens * query_tokens.shape[1] * nb * ns * LANES
    return pl.pallas_call(
        block_max_kernel,
        out_shape=jax.ShapeDtypeStruct((tokens, nb), jnp.float32),
        in_specs=[
            pl.BlockSpec(memory_space=pltpu.SMEM),
            pl.BlockSpec(memory_space=pltpu.SMEM),
            pl.BlockSpec(memory_space=pltpu.SMEM),
            pl.BlockSpec(memory_space=pltpu.VMEM),
            pl.BlockSpec(memory_space=pltpu.VMEM),
            pl.BlockSpec(memory_space=pltpu.VMEM),
        ],
        out_specs=pl.BlockSpec(memory_space=pltpu.VMEM),
        scratch_shapes=[pltpu.VMEM((tokens, LANES), jnp.float32)],
        compiler_params=pltpu.CompilerParams(vmem_limit_bytes=48 * 1024 * 1024),
        cost_estimate=pl.CostEstimate(
            flops=flops, transcendentals=0,
            bytes_accessed=own.size * 2 + query_tokens.size * 2 + tile_mask.size * 4),
    )(tile_ids.reshape(nb * ns), slot_use.reshape(nb * ns), block_has, query_tokens, own, tile_mask)


def local(query_tokens, centroids, tile_ids, tile_count, tile_mask):
    nb, ns = tile_ids.shape[0], tile_ids.shape[2]
    rows = centroids.shape[0]
    per_dev = rows // LANES
    chips = CHIP_X * CHIP_Y
    core = lax.axis_index("core")
    ids = tile_ids.reshape(nb, ns)
    mask = tile_mask.reshape(nb, ns, LANES)
    slot = lax.broadcasted_iota(jnp.int32, (nb, ns), 1)
    live = ((slot < tile_count.reshape(nb, 1)) & jnp.any(mask > 0, axis=2)).astype(jnp.int32)
    p_ids, p_live, p_mask = lax.ppermute((ids, live, mask), "core", [(0, 1), (1, 0)])
    first = core == 0
    all_ids = jnp.where(first, jnp.concatenate([ids, p_ids]), jnp.concatenate([p_ids, ids]))
    all_live = jnp.where(first, jnp.concatenate([live, p_live]), jnp.concatenate([p_live, live]))
    all_mask = jnp.where(first, jnp.concatenate([mask, p_mask]), jnp.concatenate([p_mask, mask]))
    owner = (jnp.clip(all_ids, 0, chips * CORES * per_dev - 1) // per_dev) % CORES
    use = ((all_live > 0) & (owner == core)).astype(jnp.int32)
    has = jnp.max(use, axis=1)
    spread = jnp.broadcast_to(centroids[None], (chips, rows, centroids.shape[1]))
    own = lax.all_to_all(spread, ("x", "y"), 0, 0, tiled=False)
    partial = block_max(query_tokens, own, all_ids, use, has, all_mask).astype(jnp.bfloat16)
    tokens = partial.shape[0]
    halves = partial.reshape(tokens, CORES, nb)
    mine_half = jnp.where(first, halves[:, 0], halves[:, 1])
    other_half = jnp.where(first, halves[:, 1], halves[:, 0])
    from_partner = lax.ppermute(other_half, "core", [(0, 1), (1, 0)])
    token_max = jnp.maximum(mine_half, from_partner)
    dense = token_max.reshape(tokens * nb // LANES, LANES)
    n_cent = lax.axis_size("cent")
    every = lax.all_to_all(jnp.broadcast_to(dense[None], (n_cent,) + dense.shape), "cent", 0, 0, tiled=False)
    full_max = jnp.max(every, axis=0).reshape(tokens, nb)
    per_query = full_max.astype(jnp.float32).reshape(QRY, QLEN, nb)
    return jnp.mean(per_query, axis=1)


def solution(mesh):
    n_cent = mesh.shape["cent"]
    split = Mesh(mesh.devices.reshape(n_cent, CHIP_X, CHIP_Y, CORES), ("cent", "x", "y", "core"))
    blk = ("x", "y", "core")
    in_specs = (
        P(),
        P(("cent",) + blk, None),
        P(blk, "cent", None),
        P(blk, "cent"),
        P(blk, "cent", None, None),
    )
    out_specs = P(None, blk)
    return jax.shard_map(local, mesh=split, in_specs=in_specs, out_specs=out_specs, check_vma=False)
```

```python
import jax
import jax.numpy as jnp
from jax import lax
from jax.experimental import pallas as pl
from jax.experimental.pallas import tpu as pltpu
from jax.sharding import Mesh
from jax.sharding import PartitionSpec as P

QLEN = 32
QRY = 16
LANES = 128
CHIP_X = 4
CHIP_Y = 4
CORES = 2


def block_max_kernel(ids_ref, use_ref, has_ref, q_ref, own_ref, m_ref, o_ref, run_ref):
    nb, ns = m_ref.shape[0], m_ref.shape[1]
    tokens = q_ref.shape[0]
    chips, rows = own_ref.shape[0], own_ref.shape[1]
    per_dev = rows // LANES
    tiles = chips * CORES * per_dev
    q = q_ref[...]
    lane = lax.broadcasted_iota(jnp.int32, (tokens, nb), 1)
    o_ref[...] = jnp.full(o_ref.shape, -jnp.inf, jnp.float32)

    def body(b, carry):
        @pl.when(has_ref[b] > 0)
        def _():
            run_ref[...] = jnp.full(run_ref.shape, -jnp.inf, jnp.float32)
            for k in range(ns):
                @pl.when(use_ref[b * ns + k] > 0)
                def _():
                    tid = jnp.clip(ids_ref[b * ns + k], 0, tiles - 1)
                    chip = (tid // per_dev) // CORES
                    start = pl.multiple_of((tid % per_dev) * LANES, LANES)
                    tile = own_ref[chip, pl.ds(start, LANES), :]
                    s = lax.dot_general(q, tile, (((1,), (1,)), ((), ())),
                                        preferred_element_type=jnp.float32)
                    s = s.astype(jnp.bfloat16).astype(jnp.float32)
                    live = m_ref[b, pl.ds(k, 1), :] > 0
                    run_ref[...] = jnp.maximum(run_ref[...], jnp.where(live, s, -jnp.inf))

            col = jnp.max(run_ref[...], axis=1, keepdims=True)
            o_ref[...] = jnp.where(lane == b, col, o_ref[...])

        return carry

    lax.fori_loop(0, nb, body, 0)


def block_max(query_tokens, own, tile_ids, slot_use, block_has, tile_mask):
    nb, ns = tile_ids.shape
    tokens = query_tokens.shape[0]
    flops = tokens * query_tokens.shape[1] * nb * ns * LANES
    return pl.pallas_call(
        block_max_kernel,
        out_shape=jax.ShapeDtypeStruct((tokens, nb), jnp.float32),
        in_specs=[
            pl.BlockSpec(memory_space=pltpu.SMEM),
            pl.BlockSpec(memory_space=pltpu.SMEM),
            pl.BlockSpec(memory_space=pltpu.SMEM),
            pl.BlockSpec(memory_space=pltpu.VMEM),
            pl.BlockSpec(memory_space=pltpu.VMEM),
            pl.BlockSpec(memory_space=pltpu.VMEM),
        ],
        out_specs=pl.BlockSpec(memory_space=pltpu.VMEM),
        scratch_shapes=[pltpu.VMEM((tokens, LANES), jnp.float32)],
        compiler_params=pltpu.CompilerParams(vmem_limit_bytes=48 * 1024 * 1024),
        cost_estimate=pl.CostEstimate(
            flops=flops, transcendentals=0,
            bytes_accessed=own.size * 2 + query_tokens.size * 2 + tile_mask.size * 4),
    )(tile_ids.reshape(nb * ns), slot_use.reshape(nb * ns), block_has, query_tokens, own, tile_mask)


def local(query_tokens, centroids, tile_ids, tile_count, tile_mask):
    nb, ns = tile_ids.shape[0], tile_ids.shape[2]
    rows = centroids.shape[0]
    per_dev = rows // LANES
    chips = CHIP_X * CHIP_Y
    core = lax.axis_index("core")
    ids = tile_ids.reshape(nb, ns)
    mask = tile_mask.reshape(nb, ns, LANES)
    slot = lax.broadcasted_iota(jnp.int32, (nb, ns), 1)
    live = ((slot < tile_count.reshape(nb, 1)) & jnp.any(mask > 0, axis=2)).astype(jnp.int32)
    p_ids, p_live, p_mask = lax.ppermute((ids, live, mask), "core", [(0, 1), (1, 0)])
    owner_limit = chips * CORES * per_dev - 1
    spread = jnp.broadcast_to(centroids[None], (chips, rows, centroids.shape[1]))
    own = lax.all_to_all(spread, ("x", "y"), 0, 0, tiled=False)

    def part(b_ids, b_live, b_mask):
        owner = (jnp.clip(b_ids, 0, owner_limit) // per_dev) % CORES
        use = ((b_live > 0) & (owner == core)).astype(jnp.int32)
        return block_max(query_tokens, own, b_ids, use, jnp.max(use, axis=1), b_mask).astype(jnp.bfloat16)

    for_partner = part(p_ids, p_live, p_mask)
    from_partner = lax.ppermute(for_partner, "core", [(0, 1), (1, 0)])
    token_max = jnp.maximum(part(ids, live, mask), from_partner)
    tokens = token_max.shape[0]
    dense = token_max.reshape(tokens * nb // LANES, LANES)
    n_cent = lax.axis_size("cent")
    every = lax.all_to_all(jnp.broadcast_to(dense[None], (n_cent,) + dense.shape), "cent", 0, 0, tiled=False)
    full_max = jnp.max(every, axis=0).reshape(tokens, nb)
    per_query = full_max.astype(jnp.float32).reshape(QRY, QLEN, nb)
    return jnp.mean(per_query, axis=1)


def solution(mesh):
    n_cent = mesh.shape["cent"]
    split = Mesh(mesh.devices.reshape(n_cent, CHIP_X, CHIP_Y, CORES), ("cent", "x", "y", "core"))
    blk = ("x", "y", "core")
    in_specs = (
        P(),
        P(("cent",) + blk, None),
        P(blk, "cent", None),
        P(blk, "cent"),
        P(blk, "cent", None, None),
    )
    out_specs = P(None, blk)
    return jax.shard_map(local, mesh=split, in_specs=in_specs, out_specs=out_specs, check_vma=False)
```

```python
import jax
import jax.numpy as jnp
from jax import lax
from jax.experimental import pallas as pl
from jax.experimental.pallas import tpu as pltpu
from jax.sharding import Mesh
from jax.sharding import PartitionSpec as P

QLEN = 32
QRY = 16
LANES = 128
CHIP_X = 4
CHIP_Y = 4
CORES = 2


def block_max_kernel(ids_ref, use_ref, has_ref, q_ref, own_ref, m_ref, o_ref, run_ref):
    nb, ns = m_ref.shape[0], m_ref.shape[1]
    tokens = q_ref.shape[0]
    chips, rows = own_ref.shape[0], own_ref.shape[1]
    per_dev = rows // LANES
    tiles = chips * CORES * per_dev
    q = q_ref[...]
    lane = lax.broadcasted_iota(jnp.int32, (tokens, nb), 1)
    o_ref[...] = jnp.full(o_ref.shape, -jnp.inf, jnp.float32)

    def body(b, carry):
        @pl.when(has_ref[b] > 0)
        def _():
            run_ref[...] = jnp.full(run_ref.shape, -jnp.inf, jnp.float32)
            for k in range(ns):
                @pl.when(use_ref[b * ns + k] > 0)
                def _():
                    tid = jnp.clip(ids_ref[b * ns + k], 0, tiles - 1)
                    chip = (tid // per_dev) // CORES
                    start = pl.multiple_of((tid % per_dev) * LANES, LANES)
                    tile = own_ref[chip, pl.ds(start, LANES), :]
                    s = lax.dot_general(q, tile, (((1,), (1,)), ((), ())),
                                        preferred_element_type=jnp.float32)
                    s = s.astype(jnp.bfloat16).astype(jnp.float32)
                    live = m_ref[b, pl.ds(k, 1), :] > 0
                    run_ref[...] = jnp.maximum(run_ref[...], jnp.where(live, s, -jnp.inf))

            col = jnp.max(run_ref[...], axis=1, keepdims=True)
            o_ref[...] = jnp.where(lane == b, col, o_ref[...])

        return carry

    lax.fori_loop(0, nb, body, 0)


def block_max(query_tokens, own, tile_ids, slot_use, block_has, tile_mask):
    nb, ns = tile_ids.shape
    tokens = query_tokens.shape[0]
    flops = tokens * query_tokens.shape[1] * nb * ns * LANES
    return pl.pallas_call(
        block_max_kernel,
        out_shape=jax.ShapeDtypeStruct((tokens, nb), jnp.float32),
        in_specs=[
            pl.BlockSpec(memory_space=pltpu.SMEM),
            pl.BlockSpec(memory_space=pltpu.SMEM),
            pl.BlockSpec(memory_space=pltpu.SMEM),
            pl.BlockSpec(memory_space=pltpu.VMEM),
            pl.BlockSpec(memory_space=pltpu.VMEM),
            pl.BlockSpec(memory_space=pltpu.VMEM),
        ],
        out_specs=pl.BlockSpec(memory_space=pltpu.VMEM),
        scratch_shapes=[pltpu.VMEM((tokens, LANES), jnp.float32)],
        compiler_params=pltpu.CompilerParams(vmem_limit_bytes=48 * 1024 * 1024),
        cost_estimate=pl.CostEstimate(
            flops=flops, transcendentals=0,
            bytes_accessed=own.size * 2 + query_tokens.size * 2 + tile_mask.size * 4),
    )(tile_ids.reshape(nb * ns), slot_use.reshape(nb * ns), block_has, query_tokens, own, tile_mask)


def fan_out_kernel(x_ref, o_ref):
    x = x_ref[...]
    for i in range(o_ref.shape[0]):
        o_ref[i] = x


def fan_out(x, copies):
    return pl.pallas_call(
        fan_out_kernel,
        out_shape=jax.ShapeDtypeStruct((copies,) + x.shape, x.dtype),
        in_specs=[pl.BlockSpec(memory_space=pltpu.VMEM)],
        out_specs=pl.BlockSpec(memory_space=pltpu.VMEM),
        compiler_params=pltpu.CompilerParams(vmem_limit_bytes=48 * 1024 * 1024),
        cost_estimate=pl.CostEstimate(flops=0, transcendentals=0, bytes_accessed=(copies + 1) * x.size * 2),
    )(x)


def local(query_tokens, centroids, tile_ids, tile_count, tile_mask):
    nb, ns = tile_ids.shape[0], tile_ids.shape[2]
    rows = centroids.shape[0]
    per_dev = rows // LANES
    chips = CHIP_X * CHIP_Y
    core = lax.axis_index("core")
    ids = tile_ids.reshape(nb, ns)
    mask = tile_mask.reshape(nb, ns, LANES)
    slot = lax.broadcasted_iota(jnp.int32, (nb, ns), 1)
    live = ((slot < tile_count.reshape(nb, 1)) & jnp.any(mask > 0, axis=2)).astype(jnp.int32)
    p_ids, p_live, p_mask = lax.ppermute((ids, live, mask), "core", [(0, 1), (1, 0)])
    owner_limit = chips * CORES * per_dev - 1
    spread = fan_out(centroids, chips)
    own = lax.all_to_all(spread, ("x", "y"), 0, 0, tiled=False)

    def part(b_ids, b_live, b_mask):
        owner = (jnp.clip(b_ids, 0, owner_limit) // per_dev) % CORES
        use = ((b_live > 0) & (owner == core)).astype(jnp.int32)
        return block_max(query_tokens, own, b_ids, use, jnp.max(use, axis=1), b_mask).astype(jnp.bfloat16)

    for_partner = part(p_ids, p_live, p_mask)
    from_partner = lax.ppermute(for_partner, "core", [(0, 1), (1, 0)])
    token_max = jnp.maximum(part(ids, live, mask), from_partner)
    tokens = token_max.shape[0]
    dense = token_max.reshape(tokens * nb // LANES, LANES)
    n_cent = lax.axis_size("cent")
    every = lax.all_to_all(jnp.broadcast_to(dense[None], (n_cent,) + dense.shape), "cent", 0, 0, tiled=False)
    full_max = jnp.max(every, axis=0).reshape(tokens, nb)
    per_query = full_max.astype(jnp.float32).reshape(QRY, QLEN, nb)
    return jnp.mean(per_query, axis=1)


def solution(mesh):
    n_cent = mesh.shape["cent"]
    split = Mesh(mesh.devices.reshape(n_cent, CHIP_X, CHIP_Y, CORES), ("cent", "x", "y", "core"))
    blk = ("x", "y", "core")
    in_specs = (
        P(),
        P(("cent",) + blk, None),
        P(blk, "cent", None),
        P(blk, "cent"),
        P(blk, "cent", None, None),
    )
    out_specs = P(None, blk)
    return jax.shard_map(local, mesh=split, in_specs=in_specs, out_specs=out_specs, check_vma=False)
```

```python
import jax
import jax.numpy as jnp
from jax import lax
from jax.experimental import pallas as pl
from jax.experimental.pallas import tpu as pltpu
from jax.sharding import Mesh
from jax.sharding import PartitionSpec as P

QLEN = 32
QRY = 16
LANES = 128
CHIP_X = 4
CHIP_Y = 4
CORES = 2


def block_max_kernel(ids_ref, use_ref, has_ref, qt_ref, own_ref, m_ref, o_ref, run_ref):
    nb, ns = m_ref.shape[0], m_ref.shape[2]
    chips, rows = own_ref.shape[0], own_ref.shape[1]
    per_dev = rows // LANES
    tiles = chips * CORES * per_dev
    qt = qt_ref[...]
    o_ref[...] = jnp.full(o_ref.shape, -jnp.inf, jnp.float32)

    def body(b, carry):
        @pl.when(has_ref[b] > 0)
        def _():
            run_ref[...] = jnp.full(run_ref.shape, -jnp.inf, jnp.float32)
            for k in range(ns):
                @pl.when(use_ref[b * ns + k] > 0)
                def _():
                    tid = jnp.clip(ids_ref[b * ns + k], 0, tiles - 1)
                    chip = (tid // per_dev) // CORES
                    start = pl.multiple_of((tid % per_dev) * LANES, LANES)
                    tile = own_ref[chip, pl.ds(start, LANES), :]
                    s = jnp.dot(tile, qt, preferred_element_type=jnp.float32)
                    s = s.astype(jnp.bfloat16).astype(jnp.float32)
                    live = m_ref[b, :, pl.ds(k, 1)] > 0
                    run_ref[...] = jnp.maximum(run_ref[...], jnp.where(live, s, -jnp.inf))

            o_ref[pl.ds(b, 1), :] = jnp.max(run_ref[...], axis=0, keepdims=True)

        return carry

    lax.fori_loop(0, nb, body, 0)


def block_max(query_t, own, tile_ids, slot_use, block_has, mask_t):
    nb, ns = tile_ids.shape
    tokens = query_t.shape[1]
    flops = tokens * query_t.shape[0] * nb * ns * LANES
    return pl.pallas_call(
        block_max_kernel,
        out_shape=jax.ShapeDtypeStruct((nb, tokens), jnp.float32),
        in_specs=[
            pl.BlockSpec(memory_space=pltpu.SMEM),
            pl.BlockSpec(memory_space=pltpu.SMEM),
            pl.BlockSpec(memory_space=pltpu.SMEM),
            pl.BlockSpec(memory_space=pltpu.VMEM),
            pl.BlockSpec(memory_space=pltpu.VMEM),
            pl.BlockSpec(memory_space=pltpu.VMEM),
        ],
        out_specs=pl.BlockSpec(memory_space=pltpu.VMEM),
        scratch_shapes=[pltpu.VMEM((LANES, tokens), jnp.float32)],
        compiler_params=pltpu.CompilerParams(vmem_limit_bytes=48 * 1024 * 1024),
        cost_estimate=pl.CostEstimate(
            flops=flops, transcendentals=0,
            bytes_accessed=own.size * 2 + query_t.size * 2 + mask_t.size * 4),
    )(tile_ids.reshape(nb * ns), slot_use.reshape(nb * ns), block_has, query_t, own, mask_t)


def local(query_tokens, centroids, tile_ids, tile_count, tile_mask):
    nb, ns = tile_ids.shape[0], tile_ids.shape[2]
    rows = centroids.shape[0]
    per_dev = rows // LANES
    chips = CHIP_X * CHIP_Y
    core = lax.axis_index("core")
    ids = tile_ids.reshape(nb, ns)
    mask = tile_mask.reshape(nb, ns, LANES)
    slot = lax.broadcasted_iota(jnp.int32, (nb, ns), 1)
    live = ((slot < tile_count.reshape(nb, 1)) & jnp.any(mask > 0, axis=2)).astype(jnp.int32)
    p_ids, p_live, p_mask = lax.ppermute((ids, live, mask), "core", [(0, 1), (1, 0)])
    owner_limit = chips * CORES * per_dev - 1
    query_t = query_tokens.T
    spread = jnp.broadcast_to(centroids[None], (chips, rows, centroids.shape[1]))
    own = lax.all_to_all(spread, ("x", "y"), 0, 0, tiled=False)

    def part(b_ids, b_live, b_mask):
        owner = (jnp.clip(b_ids, 0, owner_limit) // per_dev) % CORES
        use = ((b_live > 0) & (owner == core)).astype(jnp.int32)
        b_mask_t = jnp.transpose(b_mask, (0, 2, 1))
        return block_max(query_t, own, b_ids, use, jnp.max(use, axis=1), b_mask_t).astype(jnp.bfloat16)

    for_partner = part(p_ids, p_live, p_mask)
    from_partner = lax.ppermute(for_partner, "core", [(0, 1), (1, 0)])
    token_max = jnp.maximum(part(ids, live, mask), from_partner)
    tokens = token_max.shape[1]
    dense = token_max.reshape(tokens * nb // LANES, LANES)
    n_cent = lax.axis_size("cent")
    every = lax.all_to_all(jnp.broadcast_to(dense[None], (n_cent,) + dense.shape), "cent", 0, 0, tiled=False)
    full_max = jnp.max(every, axis=0).reshape(nb, tokens)
    per_query = full_max.astype(jnp.float32).reshape(nb, QRY, QLEN)
    return jnp.mean(per_query, axis=2).T


def solution(mesh):
    n_cent = mesh.shape["cent"]
    split = Mesh(mesh.devices.reshape(n_cent, CHIP_X, CHIP_Y, CORES), ("cent", "x", "y", "core"))
    blk = ("x", "y", "core")
    in_specs = (
        P(),
        P(("cent",) + blk, None),
        P(blk, "cent", None),
        P(blk, "cent"),
        P(blk, "cent", None, None),
    )
    out_specs = P(None, blk)
    return jax.shard_map(local, mesh=split, in_specs=in_specs, out_specs=out_specs, check_vma=False)
```

```python
import jax
import jax.numpy as jnp
from jax import lax
from jax.experimental import pallas as pl
from jax.experimental.pallas import tpu as pltpu
from jax.sharding import Mesh
from jax.sharding import PartitionSpec as P

QLEN = 32
QRY = 16
LANES = 128
CHIP_X = 4
CHIP_Y = 4
CORES = 2
HALVES = 2
TILES = 128


def block_max_kernel(ids_ref, use_ref, has_ref, q_ref, own_ref, m_ref, o_ref, run_ref):
    nb, ns = m_ref.shape[0], m_ref.shape[1]
    tokens = q_ref.shape[0]
    chips, rows = own_ref.shape[0], own_ref.shape[1]
    per_dev = rows // LANES
    tiles = TILES
    q = q_ref[...]
    lane = lax.broadcasted_iota(jnp.int32, (tokens, nb), 1)
    o_ref[...] = jnp.full(o_ref.shape, -jnp.inf, jnp.float32)

    def body(b, carry):
        @pl.when(has_ref[b] > 0)
        def _():
            run_ref[...] = jnp.full(run_ref.shape, -jnp.inf, jnp.float32)
            for k in range(ns):
                @pl.when(use_ref[b * ns + k] > 0)
                def _():
                    tid = jnp.clip(ids_ref[b * ns + k], 0, tiles - 1)
                    chip = (tid // per_dev // CORES) % chips
                    start = pl.multiple_of((tid % per_dev) * LANES, LANES)
                    tile = own_ref[chip, pl.ds(start, LANES), :]
                    s = lax.dot_general(q, tile, (((1,), (1,)), ((), ())),
                                        preferred_element_type=jnp.float32)
                    s = s.astype(jnp.bfloat16).astype(jnp.float32)
                    live = m_ref[b, pl.ds(k, 1), :] > 0
                    run_ref[...] = jnp.maximum(run_ref[...], jnp.where(live, s, -jnp.inf))

            col = jnp.max(run_ref[...], axis=1, keepdims=True)
            o_ref[...] = jnp.where(lane == b, col, o_ref[...])

        return carry

    lax.fori_loop(0, nb, body, 0)


def block_max(query_tokens, own, tile_ids, slot_use, block_has, tile_mask):
    nb, ns = tile_ids.shape
    tokens = query_tokens.shape[0]
    flops = tokens * query_tokens.shape[1] * nb * ns * LANES
    return pl.pallas_call(
        block_max_kernel,
        out_shape=jax.ShapeDtypeStruct((tokens, nb), jnp.float32),
        in_specs=[
            pl.BlockSpec(memory_space=pltpu.SMEM),
            pl.BlockSpec(memory_space=pltpu.SMEM),
            pl.BlockSpec(memory_space=pltpu.SMEM),
            pl.BlockSpec(memory_space=pltpu.VMEM),
            pl.BlockSpec(memory_space=pltpu.VMEM),
            pl.BlockSpec(memory_space=pltpu.VMEM),
        ],
        out_specs=pl.BlockSpec(memory_space=pltpu.VMEM),
        scratch_shapes=[pltpu.VMEM((tokens, LANES), jnp.float32)],
        compiler_params=pltpu.CompilerParams(vmem_limit_bytes=48 * 1024 * 1024),
        cost_estimate=pl.CostEstimate(
            flops=flops, transcendentals=0,
            bytes_accessed=own.size * 2 + query_tokens.size * 2 + tile_mask.size * 4),
    )(tile_ids.reshape(nb * ns), slot_use.reshape(nb * ns), block_has, query_tokens, own, tile_mask)


def local(query_tokens, centroids, tile_ids, tile_count, tile_mask):
    nb, ns = tile_ids.shape[0], tile_ids.shape[2]
    rows = centroids.shape[0]
    per_dev = rows // LANES
    chips = (CHIP_X // HALVES) * CHIP_Y
    group = HALVES * CORES
    half = lax.axis_index("xh")
    core = lax.axis_index("core")
    me = half * CORES + core
    ids = tile_ids.reshape(nb, ns)
    mask = tile_mask.reshape(nb, ns, LANES)
    slot = lax.broadcasted_iota(jnp.int32, (nb, ns), 1)
    live = ((slot < tile_count.reshape(nb, 1)) & jnp.any(mask > 0, axis=2)).astype(jnp.int32)
    pad = jnp.zeros((nb, 2, LANES), jnp.int32)
    info = jnp.concatenate([mask, pad.at[:, 0, :ns].set(ids).at[:, 1, :ns].set(live)], axis=1)
    by_core = lax.ppermute(info, "core", [(0, 1), (1, 0)])
    by_half = lax.ppermute(info, "xh", [(0, 1), (1, 0)])
    by_both = lax.ppermute(info, ("xh", "core"), [(0, 3), (3, 0), (1, 2), (2, 1)])
    spread = jnp.broadcast_to(centroids[None], (chips, rows, centroids.shape[1]))
    own = lax.all_to_all(spread, ("xl", "y"), 0, 0, tiled=False)
    members = []
    for j in range(group):
        same_half = (j // CORES) == half
        same_core = (j % CORES) == core
        members.append(jnp.where(same_half, jnp.where(same_core, info, by_core),
                                 jnp.where(same_core, by_half, by_both)))
    every_info = jnp.concatenate(members, axis=0)
    all_mask = every_info[:, :ns, :]
    all_ids = every_info[:, ns, :ns]
    all_live = every_info[:, ns + 1, :ns]
    dev = jnp.clip(all_ids, 0, TILES - 1) // per_dev
    mine = ((dev // (CHIP_Y * CORES * (CHIP_X // HALVES))) == half) & ((dev % CORES) == core)
    use = ((all_live > 0) & mine).astype(jnp.int32)
    partial = block_max(query_tokens, own, all_ids, use, jnp.max(use, axis=1), all_mask).astype(jnp.bfloat16)
    tokens = partial.shape[0]
    chunks = partial.reshape(tokens, group, nb).transpose(1, 0, 2).reshape(group, tokens * nb // LANES, LANES)
    back = lax.all_to_all(chunks, ("xh", "core"), 0, 0, tiled=False)
    dense = jnp.max(back, axis=0)
    n_cent = lax.axis_size("cent")
    every = lax.all_to_all(jnp.broadcast_to(dense[None], (n_cent,) + dense.shape), "cent", 0, 0, tiled=False)
    full_max = jnp.max(every, axis=0).reshape(tokens, nb)
    per_query = full_max.astype(jnp.float32).reshape(QRY, QLEN, nb)
    return jnp.mean(per_query, axis=1)


def solution(mesh):
    n_cent = mesh.shape["cent"]
    split = Mesh(mesh.devices.reshape(n_cent, HALVES, CHIP_X // HALVES, CHIP_Y, CORES),
                 ("cent", "xh", "xl", "y", "core"))
    blk = ("xh", "xl", "y", "core")
    in_specs = (
        P(),
        P(("cent",) + blk, None),
        P(blk, "cent", None),
        P(blk, "cent"),
        P(blk, "cent", None, None),
    )
    out_specs = P(None, blk)
    return jax.shard_map(local, mesh=split, in_specs=in_specs, out_specs=out_specs, check_vma=False)
```

```python
import jax
import jax.numpy as jnp
from jax import lax
from jax.experimental import pallas as pl
from jax.experimental.pallas import tpu as pltpu
from jax.sharding import Mesh
from jax.sharding import PartitionSpec as P

QLEN = 32
QRY = 16
LANES = 128
CHIP_X = 4
CHIP_Y = 4
CORES = 2
HALVES = 2
TILES = 128


def block_max_kernel(ids_ref, use_ref, has_ref, q_ref, own_ref, m_ref, o_ref, run_ref):
    nb, ns = m_ref.shape[0], m_ref.shape[1]
    tokens = q_ref.shape[0]
    chips, rows = own_ref.shape[0], own_ref.shape[1]
    per_dev = rows // LANES
    tiles = TILES
    q = q_ref[...]
    lane = lax.broadcasted_iota(jnp.int32, (tokens, nb), 1)
    o_ref[...] = jnp.full(o_ref.shape, -jnp.inf, jnp.float32)

    def body(b, carry):
        @pl.when(has_ref[b] > 0)
        def _():
            run_ref[...] = jnp.full(run_ref.shape, -jnp.inf, jnp.float32)
            for k in range(ns):
                @pl.when(use_ref[b * ns + k] > 0)
                def _():
                    tid = jnp.clip(ids_ref[b * ns + k], 0, tiles - 1)
                    chip = (tid // per_dev // CORES) % chips
                    start = pl.multiple_of((tid % per_dev) * LANES, LANES)
                    tile = own_ref[chip, pl.ds(start, LANES), :]
                    s = lax.dot_general(q, tile, (((1,), (1,)), ((), ())),
                                        preferred_element_type=jnp.float32)
                    s = s.astype(jnp.bfloat16).astype(jnp.float32)
                    live = m_ref[b, pl.ds(k, 1), :] > 0
                    run_ref[...] = jnp.maximum(run_ref[...], jnp.where(live, s, -jnp.inf))

            col = jnp.max(run_ref[...], axis=1, keepdims=True)
            o_ref[...] = jnp.where(lane == b, col, o_ref[...])

        return carry

    lax.fori_loop(0, nb, body, 0)


def block_max(query_tokens, own, tile_ids, slot_use, block_has, tile_mask):
    nb, ns = tile_ids.shape
    tokens = query_tokens.shape[0]
    flops = tokens * query_tokens.shape[1] * nb * ns * LANES
    return pl.pallas_call(
        block_max_kernel,
        out_shape=jax.ShapeDtypeStruct((tokens, nb), jnp.float32),
        in_specs=[
            pl.BlockSpec(memory_space=pltpu.SMEM),
            pl.BlockSpec(memory_space=pltpu.SMEM),
            pl.BlockSpec(memory_space=pltpu.SMEM),
            pl.BlockSpec(memory_space=pltpu.VMEM),
            pl.BlockSpec(memory_space=pltpu.VMEM),
            pl.BlockSpec(memory_space=pltpu.VMEM),
        ],
        out_specs=pl.BlockSpec(memory_space=pltpu.VMEM),
        scratch_shapes=[pltpu.VMEM((tokens, LANES), jnp.float32)],
        compiler_params=pltpu.CompilerParams(vmem_limit_bytes=48 * 1024 * 1024),
        cost_estimate=pl.CostEstimate(
            flops=flops, transcendentals=0,
            bytes_accessed=own.size * 2 + query_tokens.size * 2 + tile_mask.size * 4),
    )(tile_ids.reshape(nb * ns), slot_use.reshape(nb * ns), block_has, query_tokens, own, tile_mask)


def local(query_tokens, centroids, tile_ids, tile_count, tile_mask):
    nb, ns = tile_ids.shape[0], tile_ids.shape[2]
    rows = centroids.shape[0]
    per_dev = rows // LANES
    chips = (CHIP_X // HALVES) * CHIP_Y
    group = HALVES * CORES
    half = lax.axis_index("xh")
    core = lax.axis_index("core")
    me = half * CORES + core
    ids = tile_ids.reshape(nb, ns)
    mask = tile_mask.reshape(nb, ns, LANES)
    slot = lax.broadcasted_iota(jnp.int32, (nb, ns), 1)
    live = ((slot < tile_count.reshape(nb, 1)) & jnp.any(mask > 0, axis=2)).astype(jnp.int32)
    pad = jnp.zeros((nb, 2, LANES), jnp.int32)
    info = jnp.concatenate([mask, pad.at[:, 0, :ns].set(ids).at[:, 1, :ns].set(live)], axis=1)
    spread = jnp.broadcast_to(centroids[None], (chips, rows, centroids.shape[1]))
    own = lax.all_to_all(spread, ("xl", "y"), 0, 0, tiled=False)
    info = info + (own[0, 0, 0] * 0).astype(jnp.int32)
    by_core = lax.ppermute(info, "core", [(0, 1), (1, 0)])
    by_half = lax.ppermute(info, "xh", [(0, 1), (1, 0)])
    by_both = lax.ppermute(info, ("xh", "core"), [(0, 3), (3, 0), (1, 2), (2, 1)])
    members = []
    for j in range(group):
        same_half = (j // CORES) == half
        same_core = (j % CORES) == core
        members.append(jnp.where(same_half, jnp.where(same_core, info, by_core),
                                 jnp.where(same_core, by_half, by_both)))
    every_info = jnp.concatenate(members, axis=0)
    all_mask = every_info[:, :ns, :]
    all_ids = every_info[:, ns, :ns]
    all_live = every_info[:, ns + 1, :ns]
    dev = jnp.clip(all_ids, 0, TILES - 1) // per_dev
    mine = ((dev // (CHIP_Y * CORES * (CHIP_X // HALVES))) == half) & ((dev % CORES) == core)
    use = ((all_live > 0) & mine).astype(jnp.int32)
    partial = block_max(query_tokens, own, all_ids, use, jnp.max(use, axis=1), all_mask).astype(jnp.bfloat16)
    tokens = partial.shape[0]
    chunks = partial.reshape(tokens, group, nb).transpose(1, 0, 2).reshape(group, tokens * nb // LANES, LANES)
    back = lax.all_to_all(chunks, ("xh", "core"), 0, 0, tiled=False)
    dense = jnp.max(back, axis=0)
    n_cent = lax.axis_size("cent")
    every = lax.all_to_all(jnp.broadcast_to(dense[None], (n_cent,) + dense.shape), "cent", 0, 0, tiled=False)
    full_max = jnp.max(every, axis=0).reshape(tokens, nb)
    per_query = full_max.astype(jnp.float32).reshape(QRY, QLEN, nb)
    return jnp.mean(per_query, axis=1)


def solution(mesh):
    n_cent = mesh.shape["cent"]
    split = Mesh(mesh.devices.reshape(n_cent, HALVES, CHIP_X // HALVES, CHIP_Y, CORES),
                 ("cent", "xh", "xl", "y", "core"))
    blk = ("xh", "xl", "y", "core")
    in_specs = (
        P(),
        P(("cent",) + blk, None),
        P(blk, "cent", None),
        P(blk, "cent"),
        P(blk, "cent", None, None),
    )
    out_specs = P(None, blk)
    return jax.shard_map(local, mesh=split, in_specs=in_specs, out_specs=out_specs, check_vma=False)
```

```python
import jax
import jax.numpy as jnp
from jax import lax
from jax.experimental import pallas as pl
from jax.experimental.pallas import tpu as pltpu
from jax.sharding import Mesh
from jax.sharding import PartitionSpec as P

QLEN = 32
QRY = 16
LANES = 128
CHIP_X = 4
CHIP_Y = 4
CORES = 2
HALVES = 2
TILES = 128


def block_max_kernel(ids_ref, use_ref, has_ref, q_ref, own_ref, m_ref, o_ref, run_ref):
    nb, ns = m_ref.shape[0], m_ref.shape[1]
    tokens = q_ref.shape[0]
    chips, rows = own_ref.shape[0], own_ref.shape[1]
    per_dev = rows // LANES
    tiles = TILES
    q = q_ref[...]
    lane = lax.broadcasted_iota(jnp.int32, (tokens, nb), 1)
    o_ref[...] = jnp.full(o_ref.shape, -jnp.inf, jnp.float32)

    def body(b, carry):
        @pl.when(has_ref[b] > 0)
        def _():
            run_ref[...] = jnp.full(run_ref.shape, -jnp.inf, jnp.float32)
            for k in range(ns):
                @pl.when(use_ref[b * ns + k] > 0)
                def _():
                    tid = jnp.clip(ids_ref[b * ns + k], 0, tiles - 1)
                    chip = (tid // per_dev // CORES) % chips
                    start = pl.multiple_of((tid % per_dev) * LANES, LANES)
                    tile = own_ref[chip, pl.ds(start, LANES), :]
                    s = lax.dot_general(q, tile, (((1,), (1,)), ((), ())),
                                        preferred_element_type=jnp.float32)
                    s = s.astype(jnp.bfloat16).astype(jnp.float32)
                    live = m_ref[b, pl.ds(k, 1), :] > 0
                    run_ref[...] = jnp.maximum(run_ref[...], jnp.where(live, s, -jnp.inf))

            col = jnp.max(run_ref[...], axis=1, keepdims=True)
            o_ref[...] = jnp.where(lane == b, col, o_ref[...])

        return carry

    lax.fori_loop(0, nb, body, 0)


def block_max(query_tokens, own, tile_ids, slot_use, block_has, tile_mask):
    nb, ns = tile_ids.shape
    tokens = query_tokens.shape[0]
    flops = tokens * query_tokens.shape[1] * nb * ns * LANES
    return pl.pallas_call(
        block_max_kernel,
        out_shape=jax.ShapeDtypeStruct((tokens, nb), jnp.float32),
        in_specs=[
            pl.BlockSpec(memory_space=pltpu.SMEM),
            pl.BlockSpec(memory_space=pltpu.SMEM),
            pl.BlockSpec(memory_space=pltpu.SMEM),
            pl.BlockSpec(memory_space=pltpu.VMEM),
            pl.BlockSpec(memory_space=pltpu.VMEM),
            pl.BlockSpec(memory_space=pltpu.VMEM),
        ],
        out_specs=pl.BlockSpec(memory_space=pltpu.VMEM),
        scratch_shapes=[pltpu.VMEM((tokens, LANES), jnp.float32)],
        compiler_params=pltpu.CompilerParams(vmem_limit_bytes=48 * 1024 * 1024),
        cost_estimate=pl.CostEstimate(
            flops=flops, transcendentals=0,
            bytes_accessed=own.size * 2 + query_tokens.size * 2 + tile_mask.size * 4),
    )(tile_ids.reshape(nb * ns), slot_use.reshape(nb * ns), block_has, query_tokens, own, tile_mask)


def local(query_tokens, centroids, tile_ids, tile_count, tile_mask):
    nb, ns = tile_ids.shape[0], tile_ids.shape[2]
    rows = centroids.shape[0]
    per_dev = rows // LANES
    chips = (CHIP_X // HALVES) * CHIP_Y
    group = HALVES * CORES
    half = lax.axis_index("xh")
    core = lax.axis_index("core")
    me = half * CORES + core
    ids = tile_ids.reshape(nb, ns)
    mask = tile_mask.reshape(nb, ns, LANES)
    slot = lax.broadcasted_iota(jnp.int32, (nb, ns), 1)
    live = ((slot < tile_count.reshape(nb, 1)) & jnp.any(mask > 0, axis=2)).astype(jnp.int32)
    pad = jnp.zeros((nb, 2, LANES), jnp.int32)
    info = jnp.concatenate([mask, pad.at[:, 0, :ns].set(ids).at[:, 1, :ns].set(live)], axis=1)
    spread = jnp.broadcast_to(centroids[None], (chips, rows, centroids.shape[1]))
    own = lax.all_to_all(spread, ("xl", "y"), 0, 0, tiled=False)
    every_info = lax.all_gather(info, ("xh", "core"), axis=0, tiled=True)
    all_mask = every_info[:, :ns, :]
    all_ids = every_info[:, ns, :ns]
    all_live = every_info[:, ns + 1, :ns]
    dev = jnp.clip(all_ids, 0, TILES - 1) // per_dev
    mine = ((dev // (CHIP_Y * CORES * (CHIP_X // HALVES))) == half) & ((dev % CORES) == core)
    use = ((all_live > 0) & mine).astype(jnp.int32)
    partial = block_max(query_tokens, own, all_ids, use, jnp.max(use, axis=1), all_mask).astype(jnp.bfloat16)
    tokens = partial.shape[0]
    chunks = partial.reshape(tokens, group, nb).transpose(1, 0, 2).reshape(group, tokens * nb // LANES, LANES)
    back = lax.all_to_all(chunks, ("xh", "core"), 0, 0, tiled=False)
    dense = jnp.max(back, axis=0)
    n_cent = lax.axis_size("cent")
    every = lax.all_to_all(jnp.broadcast_to(dense[None], (n_cent,) + dense.shape), "cent", 0, 0, tiled=False)
    full_max = jnp.max(every, axis=0).reshape(tokens, nb)
    per_query = full_max.astype(jnp.float32).reshape(QRY, QLEN, nb)
    return jnp.mean(per_query, axis=1)


def solution(mesh):
    n_cent = mesh.shape["cent"]
    split = Mesh(mesh.devices.reshape(n_cent, HALVES, CHIP_X // HALVES, CHIP_Y, CORES),
                 ("cent", "xh", "xl", "y", "core"))
    blk = ("xh", "xl", "y", "core")
    in_specs = (
        P(),
        P(("cent",) + blk, None),
        P(blk, "cent", None),
        P(blk, "cent"),
        P(blk, "cent", None, None),
    )
    out_specs = P(None, blk)
    return jax.shard_map(local, mesh=split, in_specs=in_specs, out_specs=out_specs, check_vma=False)
```

```python
import jax
import jax.numpy as jnp
from jax import lax
from jax.experimental import pallas as pl
from jax.experimental.pallas import tpu as pltpu
from jax.sharding import Mesh
from jax.sharding import PartitionSpec as P

QLEN = 32
QRY = 16
LANES = 128
CHIP_X = 4
CHIP_Y = 4
CORES = 2
HALVES = 2
TILES = 128


def block_max_kernel(ids_ref, use_ref, has_ref, q_ref, own_ref, m_ref, o_ref, run_ref):
    nb, ns = m_ref.shape[0], m_ref.shape[1]
    tokens = q_ref.shape[0]
    chips, rows = own_ref.shape[0], own_ref.shape[1]
    per_dev = rows // LANES
    tiles = TILES
    q = q_ref[...]
    lane = lax.broadcasted_iota(jnp.int32, (tokens, nb), 1)
    o_ref[...] = jnp.full(o_ref.shape, -jnp.inf, jnp.float32)

    def body(b, carry):
        @pl.when(has_ref[b] > 0)
        def _():
            run_ref[...] = jnp.full(run_ref.shape, -jnp.inf, jnp.float32)
            for k in range(ns):
                @pl.when(use_ref[b * ns + k] > 0)
                def _():
                    tid = jnp.clip(ids_ref[b * ns + k], 0, tiles - 1)
                    chip = (tid // per_dev // CORES) % chips
                    start = pl.multiple_of((tid % per_dev) * LANES, LANES)
                    tile = own_ref[chip, pl.ds(start, LANES), :]
                    s = lax.dot_general(q, tile, (((1,), (1,)), ((), ())),
                                        preferred_element_type=jnp.float32)
                    s = s.astype(jnp.bfloat16).astype(jnp.float32)
                    live = m_ref[b, pl.ds(k, 1), :] > 0
                    run_ref[...] = jnp.maximum(run_ref[...], jnp.where(live, s, -jnp.inf))

            col = jnp.max(run_ref[...], axis=1, keepdims=True)
            o_ref[...] = jnp.where(lane == b, col, o_ref[...])

        return carry

    lax.fori_loop(0, nb, body, 0)


def block_max(query_tokens, own, tile_ids, slot_use, block_has, tile_mask):
    nb, ns = tile_ids.shape
    tokens = query_tokens.shape[0]
    flops = tokens * query_tokens.shape[1] * nb * ns * LANES
    return pl.pallas_call(
        block_max_kernel,
        out_shape=jax.ShapeDtypeStruct((tokens, nb), jnp.float32),
        in_specs=[
            pl.BlockSpec(memory_space=pltpu.SMEM),
            pl.BlockSpec(memory_space=pltpu.SMEM),
            pl.BlockSpec(memory_space=pltpu.SMEM),
            pl.BlockSpec(memory_space=pltpu.VMEM),
            pl.BlockSpec(memory_space=pltpu.VMEM),
            pl.BlockSpec(memory_space=pltpu.VMEM),
        ],
        out_specs=pl.BlockSpec(memory_space=pltpu.VMEM),
        scratch_shapes=[pltpu.VMEM((tokens, LANES), jnp.float32)],
        compiler_params=pltpu.CompilerParams(vmem_limit_bytes=48 * 1024 * 1024),
        cost_estimate=pl.CostEstimate(
            flops=flops, transcendentals=0,
            bytes_accessed=own.size * 2 + query_tokens.size * 2 + tile_mask.size * 4),
    )(tile_ids.reshape(nb * ns), slot_use.reshape(nb * ns), block_has, query_tokens, own, tile_mask)


def local(query_tokens, centroids, tile_ids, tile_count, tile_mask):
    nb, ns = tile_ids.shape[0], tile_ids.shape[2]
    rows = centroids.shape[0]
    per_dev = rows // LANES
    chips = (CHIP_X // HALVES) * CHIP_Y
    group = HALVES * CORES
    half = lax.axis_index("xh")
    core = lax.axis_index("core")
    me = half * CORES + core
    ids = tile_ids.reshape(nb, ns)
    mask = tile_mask.reshape(nb, ns, LANES)
    slot = lax.broadcasted_iota(jnp.int32, (nb, ns), 1)
    live = ((slot < tile_count.reshape(nb, 1)) & jnp.any(mask > 0, axis=2)).astype(jnp.int32)
    pad = jnp.zeros((nb, 2, LANES), jnp.int32)
    info = jnp.concatenate([mask, pad.at[:, 0, :ns].set(ids).at[:, 1, :ns].set(live)], axis=1).astype(jnp.bfloat16)
    spread = jnp.broadcast_to(centroids[None], (chips, rows, centroids.shape[1]))
    own = lax.all_to_all(spread, ("xl", "y"), 0, 0, tiled=False)
    every_info = lax.all_gather(info, ("xh", "core"), axis=0, tiled=True)
    all_mask = every_info[:, :ns, :].astype(jnp.int32)
    all_ids = every_info[:, ns, :ns].astype(jnp.int32)
    all_live = every_info[:, ns + 1, :ns].astype(jnp.int32)
    dev = jnp.clip(all_ids, 0, TILES - 1) // per_dev
    mine = ((dev // (CHIP_Y * CORES * (CHIP_X // HALVES))) == half) & ((dev % CORES) == core)
    use = ((all_live > 0) & mine).astype(jnp.int32)
    partial = block_max(query_tokens, own, all_ids, use, jnp.max(use, axis=1), all_mask).astype(jnp.bfloat16)
    tokens = partial.shape[0]
    chunks = partial.reshape(tokens, group, nb).transpose(1, 0, 2).reshape(group, tokens * nb // LANES, LANES)
    back = lax.all_to_all(chunks, ("xh", "core"), 0, 0, tiled=False)
    dense = jnp.max(back, axis=0)
    n_cent = lax.axis_size("cent")
    every = lax.all_to_all(jnp.broadcast_to(dense[None], (n_cent,) + dense.shape), "cent", 0, 0, tiled=False)
    full_max = jnp.max(every, axis=0).reshape(tokens, nb)
    per_query = full_max.astype(jnp.float32).reshape(QRY, QLEN, nb)
    return jnp.mean(per_query, axis=1)


def solution(mesh):
    n_cent = mesh.shape["cent"]
    split = Mesh(mesh.devices.reshape(n_cent, HALVES, CHIP_X // HALVES, CHIP_Y, CORES),
                 ("cent", "xh", "xl", "y", "core"))
    blk = ("xh", "xl", "y", "core")
    in_specs = (
        P(),
        P(("cent",) + blk, None),
        P(blk, "cent", None),
        P(blk, "cent"),
        P(blk, "cent", None, None),
    )
    out_specs = P(None, blk)
    return jax.shard_map(local, mesh=split, in_specs=in_specs, out_specs=out_specs, check_vma=False)
```

```python
import jax
import jax.numpy as jnp
from jax import lax
from jax.experimental import pallas as pl
from jax.experimental.pallas import tpu as pltpu
from jax.sharding import Mesh
from jax.sharding import PartitionSpec as P

QLEN = 32
QRY = 16
LANES = 128
CHIP_X = 4
CHIP_Y = 4
CORES = 2
HALVES = 2
TILES = 128


def block_max_kernel(ids_ref, use_ref, has_ref, q_ref, own_ref, m_ref, o_ref, run_ref):
    nb, ns = m_ref.shape[0], m_ref.shape[1]
    tokens = q_ref.shape[0]
    chips, rows = own_ref.shape[0], own_ref.shape[1]
    per_dev = rows // LANES
    tiles = TILES
    q = q_ref[...]
    lane = lax.broadcasted_iota(jnp.int32, (tokens, nb), 1)
    o_ref[...] = jnp.full(o_ref.shape, -jnp.inf, jnp.float32)

    def body(b, carry):
        @pl.when(has_ref[b] > 0)
        def _():
            run_ref[...] = jnp.full(run_ref.shape, -jnp.inf, jnp.float32)
            for k in range(ns):
                @pl.when(use_ref[b * ns + k] > 0)
                def _():
                    tid = jnp.clip(ids_ref[b * ns + k], 0, tiles - 1)
                    dev = tid // per_dev
                    chip = (dev // (CORES * CHIP_Y * HALVES)) * CHIP_Y + (dev // CORES) % CHIP_Y
                    start = pl.multiple_of((tid % per_dev) * LANES, LANES)
                    tile = own_ref[chip, pl.ds(start, LANES), :]
                    s = lax.dot_general(q, tile, (((1,), (1,)), ((), ())),
                                        preferred_element_type=jnp.float32)
                    s = s.astype(jnp.bfloat16).astype(jnp.float32)
                    live = m_ref[b, pl.ds(k, 1), :] > 0
                    run_ref[...] = jnp.maximum(run_ref[...], jnp.where(live, s, -jnp.inf))

            col = jnp.max(run_ref[...], axis=1, keepdims=True)
            o_ref[...] = jnp.where(lane == b, col, o_ref[...])

        return carry

    lax.fori_loop(0, nb, body, 0)


def block_max(query_tokens, own, tile_ids, slot_use, block_has, tile_mask):
    nb, ns = tile_ids.shape
    tokens = query_tokens.shape[0]
    flops = tokens * query_tokens.shape[1] * nb * ns * LANES
    return pl.pallas_call(
        block_max_kernel,
        out_shape=jax.ShapeDtypeStruct((tokens, nb), jnp.float32),
        in_specs=[
            pl.BlockSpec(memory_space=pltpu.SMEM),
            pl.BlockSpec(memory_space=pltpu.SMEM),
            pl.BlockSpec(memory_space=pltpu.SMEM),
            pl.BlockSpec(memory_space=pltpu.VMEM),
            pl.BlockSpec(memory_space=pltpu.VMEM),
            pl.BlockSpec(memory_space=pltpu.VMEM),
        ],
        out_specs=pl.BlockSpec(memory_space=pltpu.VMEM),
        scratch_shapes=[pltpu.VMEM((tokens, LANES), jnp.float32)],
        compiler_params=pltpu.CompilerParams(vmem_limit_bytes=48 * 1024 * 1024),
        cost_estimate=pl.CostEstimate(
            flops=flops, transcendentals=0,
            bytes_accessed=own.size * 2 + query_tokens.size * 2 + tile_mask.size * 4),
    )(tile_ids.reshape(nb * ns), slot_use.reshape(nb * ns), block_has, query_tokens, own, tile_mask)


def local(query_tokens, centroids, tile_ids, tile_count, tile_mask):
    nb, ns = tile_ids.shape[0], tile_ids.shape[2]
    rows = centroids.shape[0]
    per_dev = rows // LANES
    chips = (CHIP_X // HALVES) * CHIP_Y
    group = HALVES * CORES
    half = lax.axis_index("xl")
    core = lax.axis_index("core")
    me = half * CORES + core
    ids = tile_ids.reshape(nb, ns)
    mask = tile_mask.reshape(nb, ns, LANES)
    slot = lax.broadcasted_iota(jnp.int32, (nb, ns), 1)
    live = ((slot < tile_count.reshape(nb, 1)) & jnp.any(mask > 0, axis=2)).astype(jnp.int32)
    pad = jnp.zeros((nb, 2, LANES), jnp.int32)
    info = jnp.concatenate([mask, pad.at[:, 0, :ns].set(ids).at[:, 1, :ns].set(live)], axis=1).astype(jnp.bfloat16)
    spread = jnp.broadcast_to(centroids[None], (chips, rows, centroids.shape[1]))
    own = lax.all_to_all(spread, ("xh", "y"), 0, 0, tiled=False)
    every_info = lax.all_gather(info, ("xl", "core"), axis=0, tiled=True)
    all_mask = every_info[:, :ns, :].astype(jnp.int32)
    all_ids = every_info[:, ns, :ns].astype(jnp.int32)
    all_live = every_info[:, ns + 1, :ns].astype(jnp.int32)
    dev = jnp.clip(all_ids, 0, TILES - 1) // per_dev
    mine = (((dev // (CHIP_Y * CORES)) % HALVES) == half) & ((dev % CORES) == core)
    use = ((all_live > 0) & mine).astype(jnp.int32)
    partial = block_max(query_tokens, own, all_ids, use, jnp.max(use, axis=1), all_mask).astype(jnp.bfloat16)
    tokens = partial.shape[0]
    chunks = partial.reshape(tokens, group, nb).transpose(1, 0, 2).reshape(group, tokens * nb // LANES, LANES)
    back = lax.all_to_all(chunks, ("xl", "core"), 0, 0, tiled=False)
    dense = jnp.max(back, axis=0)
    n_cent = lax.axis_size("cent")
    every = lax.all_to_all(jnp.broadcast_to(dense[None], (n_cent,) + dense.shape), "cent", 0, 0, tiled=False)
    full_max = jnp.max(every, axis=0).reshape(tokens, nb)
    per_query = full_max.astype(jnp.float32).reshape(QRY, QLEN, nb)
    return jnp.mean(per_query, axis=1)


def solution(mesh):
    n_cent = mesh.shape["cent"]
    split = Mesh(mesh.devices.reshape(n_cent, HALVES, CHIP_X // HALVES, CHIP_Y, CORES),
                 ("cent", "xh", "xl", "y", "core"))
    blk = ("xh", "xl", "y", "core")
    in_specs = (
        P(),
        P(("cent",) + blk, None),
        P(blk, "cent", None),
        P(blk, "cent"),
        P(blk, "cent", None, None),
    )
    out_specs = P(None, blk)
    return jax.shard_map(local, mesh=split, in_specs=in_specs, out_specs=out_specs, check_vma=False)
```

```python
import jax
import jax.numpy as jnp
from jax import lax
from jax.experimental import pallas as pl
from jax.experimental.pallas import tpu as pltpu
from jax.sharding import Mesh
from jax.sharding import PartitionSpec as P

QLEN = 32
QRY = 16
LANES = 128
CHIP_X = 4
CHIP_Y = 4
CORES = 2
HALVES = 2
TILES = 128


def block_max_kernel(ids_ref, use_ref, has_ref, q_ref, own_ref, m_ref, o_ref, run_ref):
    nb, ns = m_ref.shape[0], m_ref.shape[1]
    tokens = q_ref.shape[0]
    chips, rows = own_ref.shape[0], own_ref.shape[1]
    per_dev = rows // LANES
    tiles = TILES
    q = q_ref[...]
    lane = lax.broadcasted_iota(jnp.int32, (tokens, nb), 1)
    o_ref[...] = jnp.full(o_ref.shape, -jnp.inf, jnp.float32)

    def body(b, carry):
        @pl.when(has_ref[b] > 0)
        def _():
            run_ref[...] = jnp.full(run_ref.shape, -jnp.inf, jnp.float32)
            for k in range(ns):
                @pl.when(use_ref[b * ns + k] > 0)
                def _():
                    tid = jnp.clip(ids_ref[b * ns + k], 0, tiles - 1)
                    dev = tid // per_dev
                    chip = (dev // (CORES * CHIP_Y * HALVES)) * CHIP_Y + (dev // CORES) % CHIP_Y
                    start = pl.multiple_of((tid % per_dev) * LANES, LANES)
                    tile = own_ref[chip, pl.ds(start, LANES), :]
                    s = lax.dot_general(q, tile, (((1,), (1,)), ((), ())),
                                        preferred_element_type=jnp.float32)
                    s = s.astype(jnp.bfloat16).astype(jnp.float32)
                    live = m_ref[b, pl.ds(k, 1), :] > 0
                    run_ref[...] = jnp.maximum(run_ref[...], jnp.where(live, s, -jnp.inf))

            col = jnp.max(run_ref[...], axis=1, keepdims=True)
            o_ref[...] = jnp.where(lane == b, col, o_ref[...])

        return carry

    lax.fori_loop(0, nb, body, 0)


def block_max(query_tokens, own, tile_ids, slot_use, block_has, tile_mask):
    nb, ns = tile_ids.shape
    tokens = query_tokens.shape[0]
    flops = tokens * query_tokens.shape[1] * nb * ns * LANES
    return pl.pallas_call(
        block_max_kernel,
        out_shape=jax.ShapeDtypeStruct((tokens, nb), jnp.float32),
        in_specs=[
            pl.BlockSpec(memory_space=pltpu.SMEM),
            pl.BlockSpec(memory_space=pltpu.SMEM),
            pl.BlockSpec(memory_space=pltpu.SMEM),
            pl.BlockSpec(memory_space=pltpu.VMEM),
            pl.BlockSpec(memory_space=pltpu.VMEM),
            pl.BlockSpec(memory_space=pltpu.VMEM),
        ],
        out_specs=pl.BlockSpec(memory_space=pltpu.VMEM),
        scratch_shapes=[pltpu.VMEM((tokens, LANES), jnp.float32)],
        compiler_params=pltpu.CompilerParams(vmem_limit_bytes=48 * 1024 * 1024),
        cost_estimate=pl.CostEstimate(
            flops=flops, transcendentals=0,
            bytes_accessed=own.size * 2 + query_tokens.size * 2 + tile_mask.size * 4),
    )(tile_ids.reshape(nb * ns), slot_use.reshape(nb * ns), block_has, query_tokens, own, tile_mask)


def local(query_tokens, centroids, tile_ids, tile_count, tile_mask):
    nb, ns = tile_ids.shape[0], tile_ids.shape[2]
    rows = centroids.shape[0]
    per_dev = rows // LANES
    chips = (CHIP_X // HALVES) * CHIP_Y
    group = HALVES * CORES
    half = lax.axis_index("xl")
    core = lax.axis_index("core")
    me = half * CORES + core
    ids = tile_ids.reshape(nb, ns)
    mask = tile_mask.reshape(nb, ns, LANES)
    slot = lax.broadcasted_iota(jnp.int32, (nb, ns), 1)
    live = ((slot < tile_count.reshape(nb, 1)) & jnp.any(mask > 0, axis=2)).astype(jnp.int32)
    pad = jnp.zeros((nb, 2, LANES), jnp.int32)
    info = jnp.concatenate([mask, pad.at[:, 0, :ns].set(ids).at[:, 1, :ns].set(live)], axis=1).astype(jnp.bfloat16)
    spread = jnp.broadcast_to(centroids[None], (chips, rows, centroids.shape[1]))
    own = lax.all_to_all(spread, ("xh", "y"), 0, 0, tiled=False)
    every_info = lax.all_gather(info, ("xl", "core"), axis=0, tiled=True)
    all_mask = every_info[:, :ns, :].astype(jnp.int32)
    all_ids = every_info[:, ns, :ns].astype(jnp.int32)
    all_live = every_info[:, ns + 1, :ns].astype(jnp.int32)
    dev = jnp.clip(all_ids, 0, TILES - 1) // per_dev
    mine = (((dev // (CHIP_Y * CORES)) % HALVES) == half) & ((dev % CORES) == core)
    others = (lax.broadcasted_iota(jnp.int32, (group, nb, ns), 0) != me).reshape(group * nb, ns)
    use = ((all_live > 0) & mine).astype(jnp.int32)
    use_others = use * others.astype(jnp.int32)
    partial = block_max(query_tokens, own, all_ids, use_others, jnp.max(use_others, axis=1), all_mask).astype(jnp.bfloat16)
    tokens = partial.shape[0]
    chunks = partial.reshape(tokens, group, nb).transpose(1, 0, 2).reshape(group, tokens * nb // LANES, LANES)
    back = lax.all_to_all(chunks, ("xl", "core"), 0, 0, tiled=False)
    own_ids = tile_ids.reshape(nb, ns)
    own_dev = jnp.clip(own_ids, 0, TILES - 1) // per_dev
    own_mine = (((own_dev // (CHIP_Y * CORES)) % HALVES) == half) & ((own_dev % CORES) == core)
    own_use = ((live > 0) & own_mine).astype(jnp.int32)
    own_part = block_max(query_tokens, own, own_ids, own_use, jnp.max(own_use, axis=1), mask).astype(jnp.bfloat16)
    dense = jnp.maximum(jnp.max(back, axis=0), own_part.reshape(tokens * nb // LANES, LANES))
    n_cent = lax.axis_size("cent")
    every = lax.all_to_all(jnp.broadcast_to(dense[None], (n_cent,) + dense.shape), "cent", 0, 0, tiled=False)
    full_max = jnp.max(every, axis=0).reshape(tokens, nb)
    per_query = full_max.astype(jnp.float32).reshape(QRY, QLEN, nb)
    return jnp.mean(per_query, axis=1)


def solution(mesh):
    n_cent = mesh.shape["cent"]
    split = Mesh(mesh.devices.reshape(n_cent, HALVES, CHIP_X // HALVES, CHIP_Y, CORES),
                 ("cent", "xh", "xl", "y", "core"))
    blk = ("xh", "xl", "y", "core")
    in_specs = (
        P(),
        P(("cent",) + blk, None),
        P(blk, "cent", None),
        P(blk, "cent"),
        P(blk, "cent", None, None),
    )
    out_specs = P(None, blk)
    return jax.shard_map(local, mesh=split, in_specs=in_specs, out_specs=out_specs, check_vma=False)
```

```python
import jax
import jax.numpy as jnp
from jax import lax
from jax.experimental import pallas as pl
from jax.experimental.pallas import tpu as pltpu
from jax.sharding import Mesh
from jax.sharding import PartitionSpec as P

QLEN = 32
QRY = 16
LANES = 128
CHIP_X = 4
CHIP_Y = 4
CORES = 2
HALVES = 2
TILES = 128


def block_max_kernel(ids_ref, use_ref, has_ref, qt_ref, own_ref, m_ref, o_ref, run_ref):
    nb, ns = m_ref.shape[0], m_ref.shape[2]
    chips, rows = own_ref.shape[0], own_ref.shape[1]
    per_dev = rows // LANES
    tiles = TILES
    qt = qt_ref[...]
    o_ref[...] = jnp.full(o_ref.shape, -jnp.inf, jnp.float32)

    def body(b, carry):
        @pl.when(has_ref[b] > 0)
        def _():
            run_ref[...] = jnp.full(run_ref.shape, -jnp.inf, jnp.float32)
            for k in range(ns):
                @pl.when(use_ref[b * ns + k] > 0)
                def _():
                    tid = jnp.clip(ids_ref[b * ns + k], 0, tiles - 1)
                    dev = tid // per_dev
                    chip = (dev // (CORES * CHIP_Y * HALVES)) * CHIP_Y + (dev // CORES) % CHIP_Y
                    start = pl.multiple_of((tid % per_dev) * LANES, LANES)
                    tile = own_ref[chip, pl.ds(start, LANES), :]
                    s = jnp.dot(tile, qt, preferred_element_type=jnp.float32)
                    s = s.astype(jnp.bfloat16).astype(jnp.float32)
                    live = m_ref[b, :, pl.ds(k, 1)] > 0
                    run_ref[...] = jnp.maximum(run_ref[...], jnp.where(live, s, -jnp.inf))

            o_ref[pl.ds(b, 1), :] = jnp.max(run_ref[...], axis=0, keepdims=True)

        return carry

    lax.fori_loop(0, nb, body, 0)


def block_max(query_t, own, tile_ids, slot_use, block_has, mask_t):
    nb, ns = tile_ids.shape
    tokens = query_t.shape[1]
    flops = tokens * query_t.shape[0] * nb * ns * LANES
    return pl.pallas_call(
        block_max_kernel,
        out_shape=jax.ShapeDtypeStruct((nb, tokens), jnp.float32),
        in_specs=[
            pl.BlockSpec(memory_space=pltpu.SMEM),
            pl.BlockSpec(memory_space=pltpu.SMEM),
            pl.BlockSpec(memory_space=pltpu.SMEM),
            pl.BlockSpec(memory_space=pltpu.VMEM),
            pl.BlockSpec(memory_space=pltpu.VMEM),
            pl.BlockSpec(memory_space=pltpu.VMEM),
        ],
        out_specs=pl.BlockSpec(memory_space=pltpu.VMEM),
        scratch_shapes=[pltpu.VMEM((LANES, tokens), jnp.float32)],
        compiler_params=pltpu.CompilerParams(vmem_limit_bytes=48 * 1024 * 1024),
        cost_estimate=pl.CostEstimate(
            flops=flops, transcendentals=0,
            bytes_accessed=own.size * 2 + query_t.size * 2 + mask_t.size * 4),
    )(tile_ids.reshape(nb * ns), slot_use.reshape(nb * ns), block_has, query_t, own, mask_t)


def local(query_tokens, centroids, tile_ids, tile_count, tile_mask):
    nb, ns = tile_ids.shape[0], tile_ids.shape[2]
    rows = centroids.shape[0]
    per_dev = rows // LANES
    chips = (CHIP_X // HALVES) * CHIP_Y
    group = HALVES * CORES
    half = lax.axis_index("xl")
    core = lax.axis_index("core")
    me = half * CORES + core
    ids = tile_ids.reshape(nb, ns)
    mask = tile_mask.reshape(nb, ns, LANES)
    slot = lax.broadcasted_iota(jnp.int32, (nb, ns), 1)
    live = ((slot < tile_count.reshape(nb, 1)) & jnp.any(mask > 0, axis=2)).astype(jnp.int32)
    pad = jnp.zeros((nb, 2, LANES), jnp.int32)
    info = jnp.concatenate([mask, pad.at[:, 0, :ns].set(ids).at[:, 1, :ns].set(live)], axis=1).astype(jnp.bfloat16)
    spread = jnp.broadcast_to(centroids[None], (chips, rows, centroids.shape[1]))
    own = lax.all_to_all(spread, ("xh", "y"), 0, 0, tiled=False)
    every_info = lax.all_gather(info, ("xl", "core"), axis=0, tiled=True)
    all_ids = every_info[:, ns, :ns].astype(jnp.int32)
    all_live = every_info[:, ns + 1, :ns].astype(jnp.int32)
    dev = jnp.clip(all_ids, 0, TILES - 1) // per_dev
    mine = (((dev // (CHIP_Y * CORES)) % HALVES) == half) & ((dev % CORES) == core)
    use = ((all_live > 0) & mine).astype(jnp.int32)
    query_t = query_tokens.T
    all_mask_t = jnp.transpose(every_info[:, :ns, :], (0, 2, 1))
    partial = block_max(query_t, own, all_ids, use, jnp.max(use, axis=1), all_mask_t).astype(jnp.bfloat16)
    tokens = partial.shape[1]
    chunks = partial.reshape(group, nb * tokens // LANES, LANES)
    back = lax.all_to_all(chunks, ("xl", "core"), 0, 0, tiled=False)
    dense = jnp.max(back, axis=0)
    n_cent = lax.axis_size("cent")
    every = lax.all_to_all(jnp.broadcast_to(dense[None], (n_cent,) + dense.shape), "cent", 0, 0, tiled=False)
    full_max = jnp.max(every, axis=0).reshape(nb, tokens)
    per_query = full_max.astype(jnp.float32).reshape(nb, QRY, QLEN)
    return jnp.mean(per_query, axis=2).T


def solution(mesh):
    n_cent = mesh.shape["cent"]
    split = Mesh(mesh.devices.reshape(n_cent, HALVES, CHIP_X // HALVES, CHIP_Y, CORES),
                 ("cent", "xh", "xl", "y", "core"))
    blk = ("xh", "xl", "y", "core")
    in_specs = (
        P(),
        P(("cent",) + blk, None),
        P(blk, "cent", None),
        P(blk, "cent"),
        P(blk, "cent", None, None),
    )
    out_specs = P(None, blk)
    return jax.shard_map(local, mesh=split, in_specs=in_specs, out_specs=out_specs, check_vma=False)
```

```python
import jax
import jax.numpy as jnp
from jax import lax
from jax.experimental import pallas as pl
from jax.experimental.pallas import tpu as pltpu
from jax.sharding import Mesh
from jax.sharding import PartitionSpec as P

QLEN = 32
QRY = 16
LANES = 128
CHIP_X = 4
CHIP_Y = 4
CORES = 2
HALVES = 2
TILES = 128


def block_max_kernel(ids_ref, use_ref, has_ref, qt_ref, own_ref, m_ref, o_ref, run_ref):
    nb, ns = m_ref.shape[0], m_ref.shape[2]
    chips, rows = own_ref.shape[0], own_ref.shape[1]
    per_dev = rows // LANES
    tiles = TILES
    qt = qt_ref[...]
    o_ref[...] = jnp.full(o_ref.shape, -jnp.inf, jnp.float32)

    def body(b, carry):
        @pl.when(has_ref[b] > 0)
        def _():
            run_ref[...] = jnp.full(run_ref.shape, -jnp.inf, jnp.float32)
            for k in range(ns):
                @pl.when(use_ref[b * ns + k] > 0)
                def _():
                    tid = jnp.clip(ids_ref[b * ns + k], 0, tiles - 1)
                    dev = tid // per_dev
                    chip = (dev // (CORES * CHIP_Y * HALVES)) * CHIP_Y + (dev // CORES) % CHIP_Y
                    start = pl.multiple_of((tid % per_dev) * LANES, LANES)
                    tile = own_ref[chip, pl.ds(start, LANES), :]
                    s = jnp.dot(tile, qt, preferred_element_type=jnp.float32)
                    s = s.astype(jnp.bfloat16).astype(jnp.float32)
                    live = m_ref[b, :, pl.ds(k, 1)] > 0
                    run_ref[...] = jnp.maximum(run_ref[...], jnp.where(live, s, -jnp.inf))

            o_ref[pl.ds(b, 1), :] = jnp.max(run_ref[...], axis=0, keepdims=True)

        return carry

    lax.fori_loop(0, nb, body, 0)


def block_max(query_t, own, tile_ids, slot_use, block_has, mask_t):
    nb, ns = tile_ids.shape
    tokens = query_t.shape[1]
    flops = tokens * query_t.shape[0] * nb * ns * LANES
    return pl.pallas_call(
        block_max_kernel,
        out_shape=jax.ShapeDtypeStruct((nb, tokens), jnp.float32),
        in_specs=[
            pl.BlockSpec(memory_space=pltpu.SMEM),
            pl.BlockSpec(memory_space=pltpu.SMEM),
            pl.BlockSpec(memory_space=pltpu.SMEM),
            pl.BlockSpec(memory_space=pltpu.VMEM),
            pl.BlockSpec(memory_space=pltpu.VMEM),
            pl.BlockSpec(memory_space=pltpu.VMEM),
        ],
        out_specs=pl.BlockSpec(memory_space=pltpu.VMEM),
        scratch_shapes=[pltpu.VMEM((LANES, tokens), jnp.float32)],
        compiler_params=pltpu.CompilerParams(vmem_limit_bytes=48 * 1024 * 1024),
        cost_estimate=pl.CostEstimate(
            flops=flops, transcendentals=0,
            bytes_accessed=own.size * 2 + query_t.size * 2 + mask_t.size * 4),
    )(tile_ids.reshape(nb * ns), slot_use.reshape(nb * ns), block_has, query_t, own, mask_t)


def local(query_tokens, centroids, tile_ids, tile_count, tile_mask):
    nb, ns = tile_ids.shape[0], tile_ids.shape[2]
    rows = centroids.shape[0]
    per_dev = rows // LANES
    chips = (CHIP_X // HALVES) * CHIP_Y
    group = HALVES * CORES
    half = lax.axis_index("xl")
    core = lax.axis_index("core")
    me = half * CORES + core
    ids = tile_ids.reshape(nb, ns)
    mask = tile_mask.reshape(nb, ns, LANES)
    slot = lax.broadcasted_iota(jnp.int32, (nb, ns), 1)
    live = ((slot < tile_count.reshape(nb, 1)) & jnp.any(mask > 0, axis=2)).astype(jnp.int32)
    pad = jnp.zeros((nb, 2, LANES), jnp.int32)
    info = jnp.concatenate([mask, pad.at[:, 0, :ns].set(ids).at[:, 1, :ns].set(live)], axis=1).astype(jnp.bfloat16)
    spread = jnp.broadcast_to(centroids[None], (chips, rows, centroids.shape[1]))
    own = lax.all_to_all(spread, ("xh", "y"), 0, 0, tiled=False)
    every_info = lax.all_gather(info, ("xl", "core"), axis=0, tiled=True)
    all_ids = every_info[:, ns, :ns].astype(jnp.int32)
    all_live = every_info[:, ns + 1, :ns].astype(jnp.int32)
    dev = jnp.clip(all_ids, 0, TILES - 1) // per_dev
    mine = (((dev // (CHIP_Y * CORES)) % HALVES) == half) & ((dev % CORES) == core)
    use = ((all_live > 0) & mine).astype(jnp.int32)
    query_t = query_tokens.T
    all_mask_t = jnp.transpose(every_info[:, :ns, :], (0, 2, 1))
    partial = block_max(query_t, own, all_ids, use, jnp.max(use, axis=1), all_mask_t).astype(jnp.bfloat16)
    tokens = partial.shape[1]
    chunks = partial.reshape(group, nb * tokens // LANES, LANES)
    back = lax.all_to_all(chunks, ("xl", "core"), 0, 0, tiled=False)
    dense = jnp.max(back, axis=0)
    n_cent = lax.axis_size("cent")
    every = lax.all_to_all(jnp.broadcast_to(dense[None], (n_cent,) + dense.shape), "cent", 0, 0, tiled=False)
    full_max = jnp.max(every, axis=0).reshape(nb, tokens)
    owner_q = lax.broadcasted_iota(jnp.int32, (QRY, tokens), 1) // QLEN
    average = jnp.where(owner_q == lax.broadcasted_iota(jnp.int32, (QRY, tokens), 0),
                        jnp.bfloat16(1.0 / QLEN), jnp.bfloat16(0))
    return lax.dot_general(average, full_max, (((1,), (1,)), ((), ())),
                           preferred_element_type=jnp.float32)


def solution(mesh):
    n_cent = mesh.shape["cent"]
    split = Mesh(mesh.devices.reshape(n_cent, HALVES, CHIP_X // HALVES, CHIP_Y, CORES),
                 ("cent", "xh", "xl", "y", "core"))
    blk = ("xh", "xl", "y", "core")
    in_specs = (
        P(),
        P(("cent",) + blk, None),
        P(blk, "cent", None),
        P(blk, "cent"),
        P(blk, "cent", None, None),
    )
    out_specs = P(None, blk)
    return jax.shard_map(local, mesh=split, in_specs=in_specs, out_specs=out_specs, check_vma=False)
```

```python
import jax
import jax.numpy as jnp
from jax import lax
from jax.experimental import pallas as pl
from jax.experimental.pallas import tpu as pltpu
from jax.sharding import Mesh
from jax.sharding import PartitionSpec as P

QLEN = 32
QRY = 16
LANES = 128
CHIP_X = 4
CHIP_Y = 4
CORES = 2
HALVES = 2
TILES = 128


def block_max_kernel(ids_ref, use_ref, has_ref, qt_ref, own_ref, m_ref, o_ref, run_ref):
    nb, ns = m_ref.shape[0], m_ref.shape[2]
    chips, rows = own_ref.shape[0], own_ref.shape[1]
    per_dev = rows // LANES
    tiles = TILES
    qt = qt_ref[...]
    o_ref[...] = jnp.full(o_ref.shape, -jnp.inf, jnp.float32)

    def body(b, carry):
        @pl.when(has_ref[b] > 0)
        def _():
            run_ref[...] = jnp.full(run_ref.shape, -jnp.inf, jnp.float32)
            for k in range(ns):
                @pl.when(use_ref[b * ns + k] > 0)
                def _():
                    tid = jnp.clip(ids_ref[b * ns + k], 0, tiles - 1)
                    dev = tid // per_dev
                    chip = (dev // 16) * 2 + (dev // 4) % 2
                    start = pl.multiple_of((tid % per_dev) * LANES, LANES)
                    tile = own_ref[chip, pl.ds(start, LANES), :]
                    s = jnp.dot(tile, qt, preferred_element_type=jnp.float32)
                    s = s.astype(jnp.bfloat16).astype(jnp.float32)
                    live = m_ref[b, :, pl.ds(k, 1)] > 0
                    run_ref[...] = jnp.maximum(run_ref[...], jnp.where(live, s, -jnp.inf))

            o_ref[pl.ds(b, 1), :] = jnp.max(run_ref[...], axis=0, keepdims=True)

        return carry

    lax.fori_loop(0, nb, body, 0)


def block_max(query_t, own, tile_ids, slot_use, block_has, mask_t):
    nb, ns = tile_ids.shape
    tokens = query_t.shape[1]
    flops = tokens * query_t.shape[0] * nb * ns * LANES
    return pl.pallas_call(
        block_max_kernel,
        out_shape=jax.ShapeDtypeStruct((nb, tokens), jnp.float32),
        in_specs=[
            pl.BlockSpec(memory_space=pltpu.SMEM),
            pl.BlockSpec(memory_space=pltpu.SMEM),
            pl.BlockSpec(memory_space=pltpu.SMEM),
            pl.BlockSpec(memory_space=pltpu.VMEM),
            pl.BlockSpec(memory_space=pltpu.VMEM),
            pl.BlockSpec(memory_space=pltpu.VMEM),
        ],
        out_specs=pl.BlockSpec(memory_space=pltpu.VMEM),
        scratch_shapes=[pltpu.VMEM((LANES, tokens), jnp.float32)],
        compiler_params=pltpu.CompilerParams(vmem_limit_bytes=48 * 1024 * 1024),
        cost_estimate=pl.CostEstimate(
            flops=flops, transcendentals=0,
            bytes_accessed=own.size * 2 + query_t.size * 2 + mask_t.size * 4),
    )(tile_ids.reshape(nb * ns), slot_use.reshape(nb * ns), block_has, query_t, own, mask_t)


def local(query_tokens, centroids, tile_ids, tile_count, tile_mask):
    nb, ns = tile_ids.shape[0], tile_ids.shape[2]
    rows = centroids.shape[0]
    per_dev = rows // LANES
    chips = HALVES * HALVES
    group = HALVES * HALVES * CORES
    xl = lax.axis_index("xl")
    yl = lax.axis_index("yl")
    core = lax.axis_index("core")
    ids = tile_ids.reshape(nb, ns)
    mask = tile_mask.reshape(nb, ns, LANES)
    slot = lax.broadcasted_iota(jnp.int32, (nb, ns), 1)
    live = ((slot < tile_count.reshape(nb, 1)) & jnp.any(mask > 0, axis=2)).astype(jnp.int32)
    pad = jnp.zeros((nb, 2, LANES), jnp.int32)
    info = jnp.concatenate([mask, pad.at[:, 0, :ns].set(ids).at[:, 1, :ns].set(live)], axis=1).astype(jnp.bfloat16)
    spread = jnp.broadcast_to(centroids[None], (chips, rows, centroids.shape[1]))
    own = lax.all_to_all(spread, ("xh", "yh"), 0, 0, tiled=False)
    members = ("xl", "yl", "core")
    every_info = lax.all_gather(info, members, axis=0, tiled=True)
    all_ids = every_info[:, ns, :ns].astype(jnp.int32)
    all_live = every_info[:, ns + 1, :ns].astype(jnp.int32)
    dev = jnp.clip(all_ids, 0, TILES - 1) // per_dev
    mine = (((dev // 8) % 2) == xl) & (((dev // 2) % 2) == yl) & ((dev % CORES) == core)
    use = ((all_live > 0) & mine).astype(jnp.int32)
    query_t = query_tokens.T
    all_mask_t = jnp.transpose(every_info[:, :ns, :], (0, 2, 1))
    partial = block_max(query_t, own, all_ids, use, jnp.max(use, axis=1), all_mask_t).astype(jnp.bfloat16)
    tokens = partial.shape[1]
    chunks = partial.reshape(group, nb * tokens // LANES, LANES)
    back = lax.all_to_all(chunks, members, 0, 0, tiled=False)
    dense = jnp.max(back, axis=0)
    n_cent = lax.axis_size("cent")
    every = lax.all_to_all(jnp.broadcast_to(dense[None], (n_cent,) + dense.shape), "cent", 0, 0, tiled=False)
    full_max = jnp.max(every, axis=0).reshape(nb, tokens)
    per_query = full_max.astype(jnp.float32).reshape(nb, QRY, QLEN)
    return jnp.mean(per_query, axis=2).T


def solution(mesh):
    n_cent = mesh.shape["cent"]
    split = Mesh(mesh.devices.reshape(n_cent, HALVES, CHIP_X // HALVES, HALVES, CHIP_Y // HALVES, CORES),
                 ("cent", "xh", "xl", "yh", "yl", "core"))
    blk = ("xh", "xl", "yh", "yl", "core")
    in_specs = (
        P(),
        P(("cent",) + blk, None),
        P(blk, "cent", None),
        P(blk, "cent"),
        P(blk, "cent", None, None),
    )
    out_specs = P(None, blk)
    return jax.shard_map(local, mesh=split, in_specs=in_specs, out_specs=out_specs, check_vma=False)
```
